256 devices in a mesh: section: 4 (over x), adapter: 2 (over core), mp: 32 (over z, y).
Axes of the slice: x: 4, y: 4, z: 8, core: 2. Of those that a mesh axis runs over, the one named last changes fastest.
Arguments:
- forward_input: bfloat16 [4, 2048, 8192], P('section', 'adapter', 'mp'), may hold values from -6 to 6
- stored_input: bfloat16 [4, 2048, 8192], P('section', 'adapter', 'mp'), may hold values from -6 to 6
- output_gradient: bfloat16 [4, 2048, 8192], P('section', 'adapter', 'mp'), may hold values from -6 to 6
- frozen_weight: bfloat16 [4, 8192, 8192], P('section', None, 'mp'), may hold values from -0.0625 to 0.0625
- adapter_down_factor: bfloat16 [4, 16, 64, 8192], P('section', 'adapter', None, 'mp'), may hold values from -0.0625 to 0.0625
- adapter_up_factor: bfloat16 [4, 16, 64, 8192], P('section', 'adapter', None, 'mp'), may hold values from -0.0625 to 0.0625
- adapter_index_list: int32 [2, 4, 16], P(None, 'section', 'adapter'), may hold values from 0 to 15, as said below
Outputs:
- fwd_out: bfloat16 [4, 2048, 8192], P('section', 'adapter', 'mp')
- grad_in: bfloat16 [4, 2048, 8192], P('section', 'adapter', 'mp')
- grad_a: bfloat16 [4, 16, 64, 8192], P('section', 'adapter', None, 'mp')
- grad_b: bfloat16 [4, 16, 64, 8192], P('section', 'adapter', None, 'mp')
The draws below stay inside these ranges and needn't reach their ends.
Inputs may be any that keep to these rules, and one draw needn't show every extreme that they name: `adapter_index_list`: owner o holds adapters o * 8 to (o + 1) * 8 - 1. Of the 8 sequences of one index of the adapter axis, for one segment and one micro-batch, at most 5 use adapters of one owner; for each segment and micro-batch one owner gets exactly 5 from every index.
All inputs are finite; a program needn't handle non-finite values.
Results may differ from the reference program's by a relative error of at most 0.013.
Values may be sent and summed in bfloat16 or wider, within the bound.
No kernel may reach another device: no remote copies, remote signals or barrier semaphores. Data moves between devices by JAX's collectives and lax.ppermute only.
A program may use at most 128 MiB of HBM per device.

```python
import jax
import jax.numpy as jnp
from jax import lax

MODEL_WIDTH = 8192
ADAPTER_RANK = 64
SEQ_LEN = 128
SEQ_DEV = 8
ADP_DEV = 8
RELAY_SEGMENTS = 4
SEGMENT_ADAPTERS = 16
SEQS = 16
MICRO_TOKENS = 2048
CAP = 5
N_MP = 32


def draw_adapter_index_list(key, part):
    owners_count = SEQS // SEQ_DEV
    slot_total = owners_count * CAP
    key_hot, key_rest = jax.random.split(key)
    hot_owner = jax.random.randint(key_hot, (2 * RELAY_SEGMENTS,), 0, owners_count)
    hot_each = jnp.repeat(hot_owner, owners_count)
    block_keys = jax.random.split(key_rest, 2 * RELAY_SEGMENTS * owners_count)

    def one_block(block_key, hot_one):
        key_score, key_shuffle, key_local = jax.random.split(block_key, 3)
        raw_score = jax.random.randint(key_score, (slot_total,), 0, 1 << 20)
        slot_ids = jnp.arange(slot_total, dtype=jnp.int32)
        scores = raw_score * slot_total + slot_ids + jnp.where(slot_ids // CAP == hot_one, 1 << 30, 0)
        top_values, chosen = lax.top_k(scores, SEQ_DEV)
        owners = (chosen // CAP).astype(jnp.int32)
        shuffle = jax.random.permutation(key_shuffle, SEQ_DEV)
        owners = owners[shuffle]
        local_ids = jax.random.randint(key_local, (SEQ_DEV,), 0, ADP_DEV)
        return owners * ADP_DEV + local_ids
    blocks_drawn = jax.vmap(one_block)(block_keys, hot_each)
    return blocks_drawn.reshape(2, RELAY_SEGMENTS, SEQS).astype(jnp.int32)


def block_levels(rng, dims, cuts, least, largest):
    def one(axis_at, blocks):
        heights = jax.random.uniform(jax.random.fold_in(jax.random.fold_in(rng, 6), axis_at), (blocks,), jnp.float32, least / len(cuts), largest / len(cuts))
        return jnp.repeat(jnp.exp(heights), dims[axis_at] // blocks).reshape((-1,) + (1,) * (len(dims) - axis_at - 1))

    loudness = one(*cuts[0])
    for cut in cuts[1:]:
        loudness = loudness * one(*cut)
    return loudness


def normal_values(own_key, dims, spread, limit, cuts=(), kind=jnp.bfloat16):
    array = spread * jax.random.normal(own_key, dims, jnp.float32)
    if cuts:
        array = array * block_levels(own_key, dims, cuts, -0.22, 0.18)
    return jnp.clip(array, -limit, limit).astype(kind)


def setup_inputs(seed: int = 0) -> dict:
    arg_keys = jax.random.split(jax.random.key(seed), 8)
    forward_input = normal_values(arg_keys[0], (RELAY_SEGMENTS, MICRO_TOKENS, MODEL_WIDTH), 1.0, 6.0, ((0, 4), (1, 2), (2, 32)))
    stored_input = normal_values(arg_keys[1], (RELAY_SEGMENTS, MICRO_TOKENS, MODEL_WIDTH), 1.0, 6.0, ((0, 4), (1, 2), (2, 32)))
    output_gradient = normal_values(arg_keys[2], (RELAY_SEGMENTS, MICRO_TOKENS, MODEL_WIDTH), 1.0, 6.0, ((0, 4), (1, 2), (2, 32)))
    frozen_weight = normal_values(arg_keys[3], (RELAY_SEGMENTS, MODEL_WIDTH, MODEL_WIDTH), MODEL_WIDTH ** -0.5, 0.0625, ((0, 4), (2, 32)))
    adapter_down_factor = normal_values(arg_keys[4], (RELAY_SEGMENTS, SEGMENT_ADAPTERS, ADAPTER_RANK, MODEL_WIDTH), MODEL_WIDTH ** -0.5, 0.0625, ((0, 4), (1, 2), (3, 32)))
    adapter_up_factor = normal_values(arg_keys[5], (RELAY_SEGMENTS, SEGMENT_ADAPTERS, ADAPTER_RANK, MODEL_WIDTH), MODEL_WIDTH ** -0.5, 0.0625, ((0, 4), (1, 2), (3, 32)))
    adapter_index_list = draw_adapter_index_list(jax.random.fold_in(arg_keys[7], 71), 0)
    return {"forward_input": forward_input, "stored_input": stored_input, "output_gradient": output_gradient, "frozen_weight": frozen_weight, "adapter_down_factor": adapter_down_factor, "adapter_up_factor": adapter_up_factor, "adapter_index_list": adapter_index_list}


adapter_scale = 2.0


def reference(forward_input, stored_input, output_gradient, frozen_weight, adapter_down_factor, adapter_up_factor, adapter_index_list):
    single_float = jnp.float32
    brain_half_float = jnp.bfloat16
    highest_accuracy = lax.Precision.HIGHEST
    width_part = MODEL_WIDTH // N_MP
    fwd_list = []
    back_list = []
    grad_a_list = []
    grad_b_list = []
    for relay_segment_index in range(RELAY_SEGMENTS):
        hidden_state = forward_input[relay_segment_index]
        weight = frozen_weight[relay_segment_index]
        down_factor_table = adapter_down_factor[relay_segment_index]
        up_factor_table = adapter_up_factor[relay_segment_index]
        forward_adapter_index = adapter_index_list[0, relay_segment_index]
        ids_back = adapter_index_list[1, relay_segment_index]
        frozen_base = jnp.dot(hidden_state, weight, preferred_element_type=single_float)
        rows_fwd = hidden_state.reshape(SEQS, SEQ_LEN, MODEL_WIDTH).astype(single_float)
        encoded_rows = jnp.einsum('msg,mog->mos', rows_fwd, down_factor_table[forward_adapter_index].astype(single_float), precision=highest_accuracy).astype(brain_half_float)
        adapter_token_rows = jnp.einsum('zpe,zpc->zec', encoded_rows.astype(single_float), up_factor_table[forward_adapter_index].astype(single_float), precision=highest_accuracy).astype(brain_half_float)
        forward_output = hidden_state.astype(single_float) + frozen_base + adapter_scale * adapter_token_rows.astype(single_float).reshape(MICRO_TOKENS, MODEL_WIDTH)
        fwd_list.append(forward_output.astype(brain_half_float))

        saved = stored_input[relay_segment_index]
        cotangent = output_gradient[relay_segment_index]
        first_sel = down_factor_table[ids_back].astype(single_float)
        second_selection = up_factor_table[ids_back].astype(single_float)
        rows_saved = saved.reshape(SEQS, SEQ_LEN, MODEL_WIDTH).astype(single_float)
        token_row_gradient = cotangent.reshape(SEQS, SEQ_LEN, MODEL_WIDTH).astype(single_float)
        encoded_backward = jnp.einsum('msg,mog->mos', rows_saved, first_sel, precision=highest_accuracy).astype(brain_half_float)
        gradient_scaled = (adapter_scale * jnp.einsum('msg,mog->mos', token_row_gradient, second_selection, precision=highest_accuracy)).astype(brain_half_float)
        back_rows = jnp.einsum('zpe,zpc->zec', gradient_scaled.astype(single_float), first_sel, precision=highest_accuracy).astype(brain_half_float)
        back_sum = jnp.zeros((MICRO_TOKENS, MODEL_WIDTH), single_float)
        for mp_index in range(N_MP):
            columns_g = cotangent[:, mp_index * width_part:(mp_index + 1) * width_part]
            columns_w = weight[:, mp_index * width_part:(mp_index + 1) * width_part]
            partial_term = lax.dot_general(columns_g, columns_w, (((1,), (1,)), ((), ())), preferred_element_type=single_float)
            back_sum = back_sum + partial_term.astype(brain_half_float).astype(single_float)
        out_back = cotangent.astype(single_float) + back_sum + back_rows.astype(single_float).reshape(MICRO_TOKENS, MODEL_WIDTH)
        back_list.append(out_back.astype(brain_half_float))

        per_seq_a = jnp.einsum('vic,vcw->viw', gradient_scaled.astype(single_float), rows_saved, precision=highest_accuracy)
        sequence_up_factor = adapter_scale * jnp.einsum('vic,vcw->viw', encoded_backward.astype(single_float), token_row_gradient, precision=highest_accuracy)
        onehot = (ids_back[:, None] == jnp.arange(SEGMENT_ADAPTERS, dtype=jnp.int32)[None, :]).astype(single_float)
        grad_a_list.append((jnp.einsum('qj,qrd->jrd', onehot, per_seq_a, precision=highest_accuracy) / SEQ_LEN).astype(brain_half_float))
        grad_b_list.append((jnp.einsum('qj,qrd->jrd', onehot, sequence_up_factor, precision=highest_accuracy) / SEQ_LEN).astype(brain_half_float))
    fwd_out = jnp.roll(jnp.stack(fwd_list), 1, axis=0)
    grad_in = jnp.roll(jnp.stack(back_list), -1, axis=0)
    return (fwd_out, grad_in, jnp.stack(grad_a_list), jnp.stack(grad_b_list))
```

```python
import jax
import jax.numpy as jnp
from jax import lax
from jax.sharding import PartitionSpec as P

adapter_scale = 2.0


def shifted(value, axis, steps):
    count = lax.axis_size(axis)
    pairs = [(source, (source + steps) % count) for source in range(count)]
    return lax.ppermute(value, axis, pairs)


def exchange(value, axis, bit):
    count = lax.axis_size(axis)
    pairs = [(source, source ^ (1 << bit)) for source in range(count)]
    return lax.ppermute(value, axis, pairs)


def halving_doubling_sum(values, axis):
    count = lax.axis_size(axis)
    levels = count.bit_length() - 1
    assert 1 << levels == count
    order = [0, 2, 1, 3, 4, 5, 6, 7, 8][:levels] if levels >= 3 else list(range(levels))
    order = [b for b in order if b < levels]
    me = lax.axis_index(axis)
    flat = jnp.concatenate([v.reshape(-1) for v in values])
    total = flat.shape[0]
    assert total % count == 0
    held = flat
    for bit in order:
        half = held.shape[0] // 2
        low, high = held[:half], held[half:]
        upper = ((me >> bit) & 1) == 1
        keep = jnp.where(upper, high, low)
        send = jnp.where(upper, low, high)
        held = keep + exchange(send, axis, bit)
    for bit in reversed(order):
        upper = ((me >> bit) & 1) == 1
        other = exchange(held, axis, bit)
        held = jnp.where(upper, jnp.concatenate([other, held]), jnp.concatenate([held, other]))
    pieces = []
    start = 0
    for v in values:
        pieces.append(held[start:start + v.size].reshape(v.shape))
        start += v.size
    return tuple(pieces)


def pack_slots(ids_row, capacity, owners_count, adapters_held):
    seq_count = ids_row.shape[0]
    owners = ids_row // adapters_held
    positions = jnp.arange(seq_count, dtype=jnp.int32)
    same_owner = owners[:, None] == owners[None, :]
    earlier = positions[None, :] < positions[:, None]
    slot_rank = jnp.sum((same_owner & earlier).astype(jnp.int32), axis=1)
    slot_index = owners * capacity + slot_rank
    slot_ids = jnp.arange(owners_count * capacity, dtype=jnp.int32)
    placing = (slot_index[None, :] == slot_ids[:, None]).astype(jnp.bfloat16)
    local_ids = ids_row % adapters_held
    pick_seq = (local_ids[:, None] == jnp.arange(adapters_held, dtype=jnp.int32)[None, :]).astype(
        jnp.bfloat16
    )
    chosen = jnp.dot(placing, pick_seq, preferred_element_type=jnp.float32).astype(jnp.bfloat16)
    return (placing, chosen.reshape(owners_count, capacity, adapters_held))


def select_slabs(chosen, table):
    return jnp.einsum("nkj,jrm->nkrm", chosen, table, preferred_element_type=jnp.float32).astype(
        jnp.bfloat16
    )


def local(
    forward_input,
    stored_input,
    output_gradient,
    frozen_weight,
    adapter_down_factor,
    adapter_up_factor,
    adapter_index_list,
):
    single_float = jnp.float32
    brain_half_float = jnp.bfloat16
    highest_accuracy = lax.Precision.HIGHEST
    owners_count = lax.axis_size("adapter")
    seq_count = adapter_index_list.shape[2]
    capacity = max(2, seq_count // owners_count + 1)
    slot_total = owners_count * capacity
    hidden_state = forward_input[0]
    saved = stored_input[0]
    cotangent = output_gradient[0]
    weight = frozen_weight[0]
    down_factor_table = adapter_down_factor[0]
    up_factor_table = adapter_up_factor[0]
    adapters_held = down_factor_table.shape[0]
    rows, width = hidden_state.shape
    seq_len = rows // seq_count
    forward_base_output = jnp.dot(
        lax.all_gather(hidden_state, "mp", axis=1, tiled=True),
        weight,
        preferred_element_type=single_float,
    )
    back_term = lax.dot_general(
        cotangent, weight, (((1,), (1,)), ((), ())), preferred_element_type=single_float
    )
    base_back = lax.psum_scatter(
        back_term.astype(jnp.bfloat16), "mp", scatter_dimension=1, tiled=True
    ).astype(jnp.float32)
    forward_placement, pick_fwd = pack_slots(
        adapter_index_list[0, 0], capacity, owners_count, adapters_held
    )
    placing_back, pick_back = pack_slots(
        adapter_index_list[1, 0], capacity, owners_count, adapters_held
    )

    def to_slots(placing, values):
        flat_rows = values.reshape(seq_count, seq_len * width)
        packed = jnp.dot(placing, flat_rows, preferred_element_type=single_float).astype(
            brain_half_float
        )
        return packed.reshape(owners_count, capacity, seq_len, width)

    def slots_gathered(placing, values):
        flat_rows = values.reshape(slot_total, seq_len * width)
        spread = lax.dot_general(
            placing, flat_rows, (((0,), (0,)), ((), ())), preferred_element_type=single_float
        )
        return spread.reshape(rows, width)

    send_fwd = to_slots(forward_placement, hidden_state)
    send_saved = to_slots(placing_back, saved)
    send_grad = to_slots(placing_back, cotangent)
    rows_fwd = lax.all_to_all(send_fwd, "adapter", split_axis=0, concat_axis=0, tiled=True)
    rows_saved = lax.all_to_all(send_saved, "adapter", split_axis=0, concat_axis=0, tiled=True)
    token_row_gradient = lax.all_to_all(
        send_grad, "adapter", split_axis=0, concat_axis=0, tiled=True
    )
    owner_fwd = lax.all_to_all(pick_fwd, "adapter", split_axis=0, concat_axis=0, tiled=True)
    owner_back = lax.all_to_all(pick_back, "adapter", split_axis=0, concat_axis=0, tiled=True)
    first_fwd = select_slabs(owner_fwd, down_factor_table)
    second_fwd = select_slabs(owner_fwd, up_factor_table)
    first_back = select_slabs(owner_back, down_factor_table)
    second_back = select_slabs(owner_back, up_factor_table)
    rank_fwd = jnp.einsum(
        "nklm,nkrm->nkrl", rows_fwd, first_fwd, preferred_element_type=single_float
    )
    rank_back = jnp.einsum(
        "nklm,nkrm->nkrl", rows_saved, first_back, preferred_element_type=single_float
    )
    rank_space_gradient = jnp.einsum(
        "nklm,nkrm->nkrl", token_row_gradient, second_back, preferred_element_type=single_float
    )
    rank_fwd, rank_back, rank_space_gradient = halving_doubling_sum(
        (rank_fwd, rank_back, rank_space_gradient), "mp"
    )
    coded_fwd = rank_fwd.astype(brain_half_float)
    encoded_backward = rank_back.astype(brain_half_float)
    gradient_scaled = (adapter_scale * rank_space_gradient).astype(brain_half_float)
    adapter_token_rows = jnp.einsum(
        "nkrl,nkrm->nklm", coded_fwd, second_fwd, preferred_element_type=single_float
    ).astype(brain_half_float)
    back_rows = jnp.einsum(
        "nkrl,nkrm->nklm", gradient_scaled, first_back, preferred_element_type=single_float
    ).astype(brain_half_float)
    adapter_home_output = lax.all_to_all(
        adapter_token_rows, "adapter", split_axis=0, concat_axis=0, tiled=True
    )
    returned_home = lax.all_to_all(back_rows, "adapter", split_axis=0, concat_axis=0, tiled=True)
    slot_down_gradient = jnp.einsum(
        "nkrl,nklm->nkrm", gradient_scaled, rows_saved, preferred_element_type=single_float
    )
    slot_up_gradient = adapter_scale * jnp.einsum(
        "nkrl,nklm->nkrm", encoded_backward, token_row_gradient, preferred_element_type=single_float
    )
    adapter_home_output, returned_home, slot_down_gradient, slot_up_gradient, owner_selection = (
        adapter_home_output,
        returned_home,
        slot_down_gradient,
        slot_up_gradient,
        owner_back,
    )
    owner_weights = owner_selection.astype(single_float)
    grad_a = (
        jnp.einsum("nkj,nkrm->jrm", owner_weights, slot_down_gradient, precision=highest_accuracy)
        / seq_len
    ).astype(brain_half_float)
    grad_b = (
        jnp.einsum("nkj,nkrm->jrm", owner_weights, slot_up_gradient, precision=highest_accuracy)
        / seq_len
    ).astype(brain_half_float)
    adapter_sequence_output = slots_gathered(forward_placement, adapter_home_output)
    back_seq = slots_gathered(placing_back, returned_home)
    forward_output = (
        hidden_state.astype(single_float)
        + forward_base_output
        + adapter_scale * adapter_sequence_output
    ).astype(brain_half_float)
    out_back = (cotangent.astype(single_float) + base_back + back_seq).astype(brain_half_float)
    fwd_next = shifted(forward_output, "section", 1)
    back_next = shifted(out_back, "section", -1)
    return (fwd_next[None], back_next[None], grad_a[None], grad_b[None])


def solution(mesh):
    in_specs = (
        P("section", "adapter", "mp"),
        P("section", "adapter", "mp"),
        P("section", "adapter", "mp"),
        P("section", None, "mp"),
        P("section", "adapter", None, "mp"),
        P("section", "adapter", None, "mp"),
        P(None, "section", "adapter"),
    )
    out_specs = (
        P("section", "adapter", "mp"),
        P("section", "adapter", "mp"),
        P("section", "adapter", None, "mp"),
        P("section", "adapter", None, "mp"),
    )
    return jax.shard_map(local, mesh=mesh, in_specs=in_specs, out_specs=out_specs, check_vma=False)
```

```python
import jax
import jax.numpy as jnp
from jax import lax
from jax.sharding import PartitionSpec as P

adapter_scale = 2.0


def shifted(value, axis, steps):
    count = lax.axis_size(axis)
    pairs = [(source, (source + steps) % count) for source in range(count)]
    return lax.ppermute(value, axis, pairs)


def exchange(value, axis, bit):
    count = lax.axis_size(axis)
    pairs = [(source, source ^ (1 << bit)) for source in range(count)]
    return lax.ppermute(value, axis, pairs)


def halving_doubling_sum(values, axis):
    count = lax.axis_size(axis)
    levels = count.bit_length() - 1
    assert 1 << levels == count
    order = [0, 2, 1, 3, 4, 5, 6, 7, 8][:levels] if levels >= 3 else list(range(levels))
    order = [b for b in order if b < levels]
    me = lax.axis_index(axis)
    flat = jnp.concatenate([v.reshape(-1) for v in values])
    total = flat.shape[0]
    assert total % count == 0
    held = flat
    for bit in order:
        half = held.shape[0] // 2
        low, high = held[:half], held[half:]
        upper = ((me >> bit) & 1) == 1
        keep = jnp.where(upper, high, low)
        send = jnp.where(upper, low, high)
        held = keep + exchange(send, axis, bit)
    for bit in reversed(order):
        upper = ((me >> bit) & 1) == 1
        other = exchange(held, axis, bit)
        held = jnp.where(upper, jnp.concatenate([other, held]), jnp.concatenate([held, other]))
    pieces = []
    start = 0
    for v in values:
        pieces.append(held[start:start + v.size].reshape(v.shape))
        start += v.size
    return tuple(pieces)


Y_RING = 4


def ring_pairs(count, z_step, y_step):
    z_count = count // Y_RING
    pairs = []
    for source in range(count):
        z, y = divmod(source, Y_RING)
        pairs.append((source, ((z + z_step) % z_count) * Y_RING + (y + y_step) % Y_RING))
    return pairs


def ring_reduce(chunks, chunk_axis, position, axis, pairs, sign):
    count = chunks.shape[chunk_axis]

    def own(offset):
        index = (position - sign * offset + 2 * count) % count
        return lax.dynamic_index_in_dim(chunks, index, axis=chunk_axis, keepdims=False).astype(
            jnp.float32
        )

    total = own(1)
    for step in range(1, count):
        arrived = lax.ppermute(total.astype(jnp.bfloat16), axis, pairs)
        total = arrived.astype(jnp.float32) + own(1 + step)
    return total


def torus_reduce_scatter(partials, axis):
    count = lax.axis_size(axis)
    z_count = count // Y_RING
    rows, columns = partials.shape
    block = columns // count
    me = lax.axis_index(axis)
    z_me, y_me = me // Y_RING, me % Y_RING
    groups = partials.reshape(4, rows // 4, z_count, Y_RING, block)
    results = []
    for group, sign in ((0, 1), (1, -1)):
        along_z = ring_reduce(groups[group], 1, z_me, axis, ring_pairs(count, sign, 0), sign)
        results.append(ring_reduce(along_z, 1, y_me, axis, ring_pairs(count, 0, sign), sign))
    for group, sign in ((2, 1), (3, -1)):
        along_y = ring_reduce(groups[group], 2, y_me, axis, ring_pairs(count, 0, sign), sign)
        results.append(ring_reduce(along_y, 1, z_me, axis, ring_pairs(count, sign, 0), sign))
    return jnp.concatenate(results, axis=0)


def pack_slots(ids_row, capacity, owners_count, adapters_held):
    seq_count = ids_row.shape[0]
    owners = ids_row // adapters_held
    positions = jnp.arange(seq_count, dtype=jnp.int32)
    same_owner = owners[:, None] == owners[None, :]
    earlier = positions[None, :] < positions[:, None]
    slot_rank = jnp.sum((same_owner & earlier).astype(jnp.int32), axis=1)
    slot_index = owners * capacity + slot_rank
    slot_ids = jnp.arange(owners_count * capacity, dtype=jnp.int32)
    placing = (slot_index[None, :] == slot_ids[:, None]).astype(jnp.bfloat16)
    local_ids = ids_row % adapters_held
    pick_seq = (local_ids[:, None] == jnp.arange(adapters_held, dtype=jnp.int32)[None, :]).astype(
        jnp.bfloat16
    )
    chosen = jnp.dot(placing, pick_seq, preferred_element_type=jnp.float32).astype(jnp.bfloat16)
    return (placing, chosen.reshape(owners_count, capacity, adapters_held))


def select_slabs(chosen, table):
    return jnp.einsum("nkj,jrm->nkrm", chosen, table, preferred_element_type=jnp.float32).astype(
        jnp.bfloat16
    )


def local(
    forward_input,
    stored_input,
    output_gradient,
    frozen_weight,
    adapter_down_factor,
    adapter_up_factor,
    adapter_index_list,
):
    single_float = jnp.float32
    brain_half_float = jnp.bfloat16
    highest_accuracy = lax.Precision.HIGHEST
    owners_count = lax.axis_size("adapter")
    seq_count = adapter_index_list.shape[2]
    capacity = max(2, seq_count // owners_count + 1)
    slot_total = owners_count * capacity
    hidden_state = forward_input[0]
    saved = stored_input[0]
    cotangent = output_gradient[0]
    weight = frozen_weight[0]
    down_factor_table = adapter_down_factor[0]
    up_factor_table = adapter_up_factor[0]
    adapters_held = down_factor_table.shape[0]
    rows, width = hidden_state.shape
    seq_len = rows // seq_count
    forward_base_output = jnp.dot(
        lax.all_gather(hidden_state, "mp", axis=1, tiled=True),
        weight,
        preferred_element_type=single_float,
    )
    back_term = lax.dot_general(
        cotangent, weight, (((1,), (1,)), ((), ())), preferred_element_type=single_float
    )
    base_back = torus_reduce_scatter(back_term.astype(jnp.bfloat16), "mp")
    forward_placement, pick_fwd = pack_slots(
        adapter_index_list[0, 0], capacity, owners_count, adapters_held
    )
    placing_back, pick_back = pack_slots(
        adapter_index_list[1, 0], capacity, owners_count, adapters_held
    )

    def to_slots(placing, values):
        flat_rows = values.reshape(seq_count, seq_len * width)
        packed = jnp.dot(placing, flat_rows, preferred_element_type=single_float).astype(
            brain_half_float
        )
        return packed.reshape(owners_count, capacity, seq_len, width)

    def slots_gathered(placing, values):
        flat_rows = values.reshape(slot_total, seq_len * width)
        spread = lax.dot_general(
            placing, flat_rows, (((0,), (0,)), ((), ())), preferred_element_type=single_float
        )
        return spread.reshape(rows, width)

    send_fwd = to_slots(forward_placement, hidden_state)
    send_saved = to_slots(placing_back, saved)
    send_grad = to_slots(placing_back, cotangent)
    rows_fwd = lax.all_to_all(send_fwd, "adapter", split_axis=0, concat_axis=0, tiled=True)
    rows_saved = lax.all_to_all(send_saved, "adapter", split_axis=0, concat_axis=0, tiled=True)
    token_row_gradient = lax.all_to_all(
        send_grad, "adapter", split_axis=0, concat_axis=0, tiled=True
    )
    owner_fwd = lax.all_to_all(pick_fwd, "adapter", split_axis=0, concat_axis=0, tiled=True)
    owner_back = lax.all_to_all(pick_back, "adapter", split_axis=0, concat_axis=0, tiled=True)
    first_fwd = select_slabs(owner_fwd, down_factor_table)
    second_fwd = select_slabs(owner_fwd, up_factor_table)
    first_back = select_slabs(owner_back, down_factor_table)
    second_back = select_slabs(owner_back, up_factor_table)
    rank_fwd = jnp.einsum(
        "nklm,nkrm->nkrl", rows_fwd, first_fwd, preferred_element_type=single_float
    )
    rank_back = jnp.einsum(
        "nklm,nkrm->nkrl", rows_saved, first_back, preferred_element_type=single_float
    )
    rank_space_gradient = jnp.einsum(
        "nklm,nkrm->nkrl", token_row_gradient, second_back, preferred_element_type=single_float
    )
    rank_fwd, rank_back, rank_space_gradient = halving_doubling_sum(
        (rank_fwd, rank_back, rank_space_gradient), "mp"
    )
    coded_fwd = rank_fwd.astype(brain_half_float)
    encoded_backward = rank_back.astype(brain_half_float)
    gradient_scaled = (adapter_scale * rank_space_gradient).astype(brain_half_float)
    adapter_token_rows = jnp.einsum(
        "nkrl,nkrm->nklm", coded_fwd, second_fwd, preferred_element_type=single_float
    ).astype(brain_half_float)
    back_rows = jnp.einsum(
        "nkrl,nkrm->nklm", gradient_scaled, first_back, preferred_element_type=single_float
    ).astype(brain_half_float)
    adapter_home_output = lax.all_to_all(
        adapter_token_rows, "adapter", split_axis=0, concat_axis=0, tiled=True
    )
    returned_home = lax.all_to_all(back_rows, "adapter", split_axis=0, concat_axis=0, tiled=True)
    slot_down_gradient = jnp.einsum(
        "nkrl,nklm->nkrm", gradient_scaled, rows_saved, preferred_element_type=single_float
    )
    slot_up_gradient = adapter_scale * jnp.einsum(
        "nkrl,nklm->nkrm", encoded_backward, token_row_gradient, preferred_element_type=single_float
    )
    adapter_home_output, returned_home, slot_down_gradient, slot_up_gradient, owner_selection = (
        adapter_home_output,
        returned_home,
        slot_down_gradient,
        slot_up_gradient,
        owner_back,
    )
    owner_weights = owner_selection.astype(single_float)
    grad_a = (
        jnp.einsum("nkj,nkrm->jrm", owner_weights, slot_down_gradient, precision=highest_accuracy)
        / seq_len
    ).astype(brain_half_float)
    grad_b = (
        jnp.einsum("nkj,nkrm->jrm", owner_weights, slot_up_gradient, precision=highest_accuracy)
        / seq_len
    ).astype(brain_half_float)
    adapter_sequence_output = slots_gathered(forward_placement, adapter_home_output)
    back_seq = slots_gathered(placing_back, returned_home)
    forward_output = (
        hidden_state.astype(single_float)
        + forward_base_output
        + adapter_scale * adapter_sequence_output
    ).astype(brain_half_float)
    out_back = (cotangent.astype(single_float) + base_back + back_seq).astype(brain_half_float)
    fwd_next = shifted(forward_output, "section", 1)
    back_next = shifted(out_back, "section", -1)
    return (fwd_next[None], back_next[None], grad_a[None], grad_b[None])


def solution(mesh):
    in_specs = (
        P("section", "adapter", "mp"),
        P("section", "adapter", "mp"),
        P("section", "adapter", "mp"),
        P("section", None, "mp"),
        P("section", "adapter", None, "mp"),
        P("section", "adapter", None, "mp"),
        P(None, "section", "adapter"),
    )
    out_specs = (
        P("section", "adapter", "mp"),
        P("section", "adapter", "mp"),
        P("section", "adapter", None, "mp"),
        P("section", "adapter", None, "mp"),
    )
    return jax.shard_map(local, mesh=mesh, in_specs=in_specs, out_specs=out_specs, check_vma=False)
```

```python
import jax
import jax.numpy as jnp
from jax import lax
from jax.sharding import PartitionSpec as P

adapter_scale = 2.0


def shifted(value, axis, steps):
    count = lax.axis_size(axis)
    pairs = [(source, (source + steps) % count) for source in range(count)]
    return lax.ppermute(value, axis, pairs)


def exchange(value, axis, bit):
    count = lax.axis_size(axis)
    pairs = [(source, source ^ (1 << bit)) for source in range(count)]
    return lax.ppermute(value, axis, pairs)


def halving_doubling_sum(values, axis):
    count = lax.axis_size(axis)
    levels = count.bit_length() - 1
    assert 1 << levels == count
    order = [0, 2, 1, 3, 4, 5, 6, 7, 8][:levels] if levels >= 3 else list(range(levels))
    order = [b for b in order if b < levels]
    me = lax.axis_index(axis)
    flat = jnp.concatenate([v.reshape(-1) for v in values])
    total = flat.shape[0]
    assert total % count == 0
    held = flat
    for bit in order:
        half = held.shape[0] // 2
        low, high = held[:half], held[half:]
        upper = ((me >> bit) & 1) == 1
        keep = jnp.where(upper, high, low)
        send = jnp.where(upper, low, high)
        held = keep + exchange(send, axis, bit)
    for bit in reversed(order):
        upper = ((me >> bit) & 1) == 1
        other = exchange(held, axis, bit)
        held = jnp.where(upper, jnp.concatenate([other, held]), jnp.concatenate([held, other]))
    pieces = []
    start = 0
    for v in values:
        pieces.append(held[start:start + v.size].reshape(v.shape))
        start += v.size
    return tuple(pieces)


Y_RING = 4


def ring_pairs(groups, count, z_step, y_step):
    z_count = count // Y_RING
    pairs = []
    for group in range(groups):
        sign = 1 if group % 2 == 0 else -1
        for source in range(count):
            z, y = divmod(source, Y_RING)
            target = ((z + sign * z_step) % z_count) * Y_RING + (y + sign * y_step) % Y_RING
            pairs.append((group * count + source, group * count + target))
    return pairs


def ring_reduce(chunks, chunk_axis, position, axes, pairs, sign):
    count = chunks.shape[chunk_axis]

    def own(offset):
        index = (position - sign * offset + 2 * count) % count
        return lax.dynamic_index_in_dim(chunks, index, axis=chunk_axis, keepdims=False).astype(
            jnp.float32
        )

    total = own(1)
    for step in range(1, count):
        arrived = lax.ppermute(total.astype(jnp.bfloat16), axes, pairs)
        total = arrived.astype(jnp.float32) + own(1 + step)
    return total


def torus_reduce_scatter(partials, ring_axis, axis):
    count = lax.axis_size(axis)
    groups = lax.axis_size(ring_axis)
    axes = (ring_axis, axis)
    sign = 1 - 2 * (lax.axis_index(ring_axis) % 2)
    me = lax.axis_index(axis)
    z_me, y_me = me // Y_RING, me % Y_RING
    z_pairs = ring_pairs(groups, count, 1, 0)
    y_pairs = ring_pairs(groups, count, 0, 1)
    along_z = ring_reduce(partials[:, :, 0], 0, z_me, axes, z_pairs, sign)
    first = ring_reduce(along_z, 0, y_me, axes, y_pairs, sign)
    along_y = ring_reduce(partials[:, :, 1], 1, y_me, axes, y_pairs, sign)
    second = ring_reduce(along_y, 0, z_me, axes, z_pairs, sign)
    return jnp.concatenate([first, second], axis=0)


def pack_slots(ids_row, capacity, owners_count, adapters_held):
    seq_count = ids_row.shape[0]
    owners = ids_row // adapters_held
    positions = jnp.arange(seq_count, dtype=jnp.int32)
    same_owner = owners[:, None] == owners[None, :]
    earlier = positions[None, :] < positions[:, None]
    slot_rank = jnp.sum((same_owner & earlier).astype(jnp.int32), axis=1)
    slot_index = owners * capacity + slot_rank
    slot_ids = jnp.arange(owners_count * capacity, dtype=jnp.int32)
    placing = (slot_index[None, :] == slot_ids[:, None]).astype(jnp.bfloat16)
    local_ids = ids_row % adapters_held
    pick_seq = (local_ids[:, None] == jnp.arange(adapters_held, dtype=jnp.int32)[None, :]).astype(
        jnp.bfloat16
    )
    chosen = jnp.dot(placing, pick_seq, preferred_element_type=jnp.float32).astype(jnp.bfloat16)
    return (placing, chosen.reshape(owners_count, capacity, adapters_held))


def select_slabs(chosen, table):
    return jnp.einsum("nkj,jrm->nkrm", chosen, table, preferred_element_type=jnp.float32).astype(
        jnp.bfloat16
    )


def local(
    forward_input,
    stored_input,
    output_gradient,
    frozen_weight,
    adapter_down_factor,
    adapter_up_factor,
    adapter_index_list,
):
    single_float = jnp.float32
    brain_half_float = jnp.bfloat16
    highest_accuracy = lax.Precision.HIGHEST
    owners_count = lax.axis_size("adapter")
    seq_count = adapter_index_list.shape[2]
    capacity = max(2, seq_count // owners_count + 1)
    slot_total = owners_count * capacity
    hidden_state = forward_input[0]
    saved = stored_input[0]
    cotangent = output_gradient[0]
    weight = frozen_weight[0]
    down_factor_table = adapter_down_factor[0]
    up_factor_table = adapter_up_factor[0]
    adapters_held = down_factor_table.shape[0]
    rows, width = hidden_state.shape
    seq_len = rows // seq_count
    forward_base_output = jnp.dot(
        lax.all_gather(hidden_state, "mp", axis=1, tiled=True),
        weight,
        preferred_element_type=single_float,
    )
    mp_count = lax.axis_size("mp")
    z_count = mp_count // Y_RING
    block = weight.shape[0] // mp_count
    weight_blocks = weight.reshape(z_count, Y_RING, block, weight.shape[1])
    back_term = jnp.einsum(
        "tc,zyic->zyti", cotangent, weight_blocks, preferred_element_type=single_float
    ).astype(jnp.bfloat16)
    base_back = torus_reduce_scatter(
        back_term.reshape(z_count, Y_RING, 2, cotangent.shape[0] // 2, block), "adapter", "mp"
    )
    forward_placement, pick_fwd = pack_slots(
        adapter_index_list[0, 0], capacity, owners_count, adapters_held
    )
    placing_back, pick_back = pack_slots(
        adapter_index_list[1, 0], capacity, owners_count, adapters_held
    )

    def to_slots(placing, values):
        flat_rows = values.reshape(seq_count, seq_len * width)
        packed = jnp.dot(placing, flat_rows, preferred_element_type=single_float).astype(
            brain_half_float
        )
        return packed.reshape(owners_count, capacity, seq_len, width)

    def slots_gathered(placing, values):
        flat_rows = values.reshape(slot_total, seq_len * width)
        spread = lax.dot_general(
            placing, flat_rows, (((0,), (0,)), ((), ())), preferred_element_type=single_float
        )
        return spread.reshape(rows, width)

    send_fwd = to_slots(forward_placement, hidden_state)
    send_saved = to_slots(placing_back, saved)
    send_grad = to_slots(placing_back, cotangent)
    rows_fwd = lax.all_to_all(send_fwd, "adapter", split_axis=0, concat_axis=0, tiled=True)
    rows_saved = lax.all_to_all(send_saved, "adapter", split_axis=0, concat_axis=0, tiled=True)
    token_row_gradient = lax.all_to_all(
        send_grad, "adapter", split_axis=0, concat_axis=0, tiled=True
    )
    owner_fwd = lax.all_to_all(pick_fwd, "adapter", split_axis=0, concat_axis=0, tiled=True)
    owner_back = lax.all_to_all(pick_back, "adapter", split_axis=0, concat_axis=0, tiled=True)
    first_fwd = select_slabs(owner_fwd, down_factor_table)
    second_fwd = select_slabs(owner_fwd, up_factor_table)
    first_back = select_slabs(owner_back, down_factor_table)
    second_back = select_slabs(owner_back, up_factor_table)
    rank_fwd = jnp.einsum(
        "nklm,nkrm->nkrl", rows_fwd, first_fwd, preferred_element_type=single_float
    )
    rank_back = jnp.einsum(
        "nklm,nkrm->nkrl", rows_saved, first_back, preferred_element_type=single_float
    )
    rank_space_gradient = jnp.einsum(
        "nklm,nkrm->nkrl", token_row_gradient, second_back, preferred_element_type=single_float
    )
    rank_fwd, rank_back, rank_space_gradient = halving_doubling_sum(
        (rank_fwd, rank_back, rank_space_gradient), "mp"
    )
    coded_fwd = rank_fwd.astype(brain_half_float)
    encoded_backward = rank_back.astype(brain_half_float)
    gradient_scaled = (adapter_scale * rank_space_gradient).astype(brain_half_float)
    adapter_token_rows = jnp.einsum(
        "nkrl,nkrm->nklm", coded_fwd, second_fwd, preferred_element_type=single_float
    ).astype(brain_half_float)
    back_rows = jnp.einsum(
        "nkrl,nkrm->nklm", gradient_scaled, first_back, preferred_element_type=single_float
    ).astype(brain_half_float)
    adapter_home_output = lax.all_to_all(
        adapter_token_rows, "adapter", split_axis=0, concat_axis=0, tiled=True
    )
    returned_home = lax.all_to_all(back_rows, "adapter", split_axis=0, concat_axis=0, tiled=True)
    slot_down_gradient = jnp.einsum(
        "nkrl,nklm->nkrm", gradient_scaled, rows_saved, preferred_element_type=single_float
    )
    slot_up_gradient = adapter_scale * jnp.einsum(
        "nkrl,nklm->nkrm", encoded_backward, token_row_gradient, preferred_element_type=single_float
    )
    adapter_home_output, returned_home, slot_down_gradient, slot_up_gradient, owner_selection = (
        adapter_home_output,
        returned_home,
        slot_down_gradient,
        slot_up_gradient,
        owner_back,
    )
    owner_weights = owner_selection.astype(single_float)
    grad_a = (
        jnp.einsum("nkj,nkrm->jrm", owner_weights, slot_down_gradient, precision=highest_accuracy)
        / seq_len
    ).astype(brain_half_float)
    grad_b = (
        jnp.einsum("nkj,nkrm->jrm", owner_weights, slot_up_gradient, precision=highest_accuracy)
        / seq_len
    ).astype(brain_half_float)
    adapter_sequence_output = slots_gathered(forward_placement, adapter_home_output)
    back_seq = slots_gathered(placing_back, returned_home)
    forward_output = (
        hidden_state.astype(single_float)
        + forward_base_output
        + adapter_scale * adapter_sequence_output
    ).astype(brain_half_float)
    out_back = (cotangent.astype(single_float) + base_back + back_seq).astype(brain_half_float)
    fwd_next = shifted(forward_output, "section", 1)
    back_next = shifted(out_back, "section", -1)
    return (fwd_next[None], back_next[None], grad_a[None], grad_b[None])


def solution(mesh):
    in_specs = (
        P("section", "adapter", "mp"),
        P("section", "adapter", "mp"),
        P("section", "adapter", "mp"),
        P("section", None, "mp"),
        P("section", "adapter", None, "mp"),
        P("section", "adapter", None, "mp"),
        P(None, "section", "adapter"),
    )
    out_specs = (
        P("section", "adapter", "mp"),
        P("section", "adapter", "mp"),
        P("section", "adapter", None, "mp"),
        P("section", "adapter", None, "mp"),
    )
    return jax.shard_map(local, mesh=mesh, in_specs=in_specs, out_specs=out_specs, check_vma=False)
```

```python
import jax
import jax.numpy as jnp
from jax import lax
from jax.sharding import PartitionSpec as P

adapter_scale = 2.0


def shifted(value, axis, steps):
    count = lax.axis_size(axis)
    pairs = [(source, (source + steps) % count) for source in range(count)]
    return lax.ppermute(value, axis, pairs)


def exchange(value, axis, bit):
    count = lax.axis_size(axis)
    pairs = [(source, source ^ (1 << bit)) for source in range(count)]
    return lax.ppermute(value, axis, pairs)


def halving_doubling_sum(values, axis):
    count = lax.axis_size(axis)
    levels = count.bit_length() - 1
    assert 1 << levels == count
    order = [0, 2, 1, 3, 4, 5, 6, 7, 8][:levels] if levels >= 3 else list(range(levels))
    order = [b for b in order if b < levels]
    me = lax.axis_index(axis)
    flat = jnp.concatenate([v.reshape(-1) for v in values])
    total = flat.shape[0]
    assert total % count == 0
    held = flat
    for bit in order:
        half = held.shape[0] // 2
        low, high = held[:half], held[half:]
        upper = ((me >> bit) & 1) == 1
        keep = jnp.where(upper, high, low)
        send = jnp.where(upper, low, high)
        held = keep + exchange(send, axis, bit)
    for bit in reversed(order):
        upper = ((me >> bit) & 1) == 1
        other = exchange(held, axis, bit)
        held = jnp.where(upper, jnp.concatenate([other, held]), jnp.concatenate([held, other]))
    pieces = []
    start = 0
    for v in values:
        pieces.append(held[start:start + v.size].reshape(v.shape))
        start += v.size
    return tuple(pieces)


Y_RING = 4


def ring_pairs(groups, count, z_step, y_step):
    z_count = count // Y_RING
    pairs = []
    for group in range(groups):
        sign = 1 if group % 2 == 0 else -1
        for source in range(count):
            z, y = divmod(source, Y_RING)
            target = ((z + sign * z_step) % z_count) * Y_RING + (y + sign * y_step) % Y_RING
            pairs.append((group * count + source, group * count + target))
    return pairs


def ring_reduce(partials, count, position, axes, pairs, sign):
    width = partials.shape[1] // count

    def own(offset):
        index = (position - sign * offset + 2 * count) % count
        return lax.dynamic_slice_in_dim(partials, index * width, width, axis=1).astype(
            jnp.float32
        )

    total = own(1)
    for step in range(1, count):
        arrived = lax.ppermute(total.astype(jnp.bfloat16), axes, pairs)
        total = arrived.astype(jnp.float32) + own(1 + step)
    return total


def torus_reduce_scatter(z_major, y_major, ring_axis, axis):
    count = lax.axis_size(axis)
    z_count = count // Y_RING
    groups = lax.axis_size(ring_axis)
    axes = (ring_axis, axis)
    sign = 1 - 2 * (lax.axis_index(ring_axis) % 2)
    me = lax.axis_index(axis)
    z_me, y_me = me // Y_RING, me % Y_RING
    z_pairs = ring_pairs(groups, count, 1, 0)
    y_pairs = ring_pairs(groups, count, 0, 1)
    along_z = ring_reduce(z_major, z_count, z_me, axes, z_pairs, sign)
    first = ring_reduce(along_z, Y_RING, y_me, axes, y_pairs, sign)
    along_y = ring_reduce(y_major, Y_RING, y_me, axes, y_pairs, sign)
    second = ring_reduce(along_y, z_count, z_me, axes, z_pairs, sign)
    return jnp.concatenate([first, second], axis=0)


def pack_slots(ids_row, capacity, owners_count, adapters_held):
    seq_count = ids_row.shape[0]
    owners = ids_row // adapters_held
    positions = jnp.arange(seq_count, dtype=jnp.int32)
    same_owner = owners[:, None] == owners[None, :]
    earlier = positions[None, :] < positions[:, None]
    slot_rank = jnp.sum((same_owner & earlier).astype(jnp.int32), axis=1)
    slot_index = owners * capacity + slot_rank
    slot_ids = jnp.arange(owners_count * capacity, dtype=jnp.int32)
    placing = (slot_index[None, :] == slot_ids[:, None]).astype(jnp.bfloat16)
    local_ids = ids_row % adapters_held
    pick_seq = (local_ids[:, None] == jnp.arange(adapters_held, dtype=jnp.int32)[None, :]).astype(
        jnp.bfloat16
    )
    chosen = jnp.dot(placing, pick_seq, preferred_element_type=jnp.float32).astype(jnp.bfloat16)
    return (placing, chosen.reshape(owners_count, capacity, adapters_held))


def select_slabs(chosen, table):
    return jnp.einsum("nkj,jrm->nkrm", chosen, table, preferred_element_type=jnp.float32).astype(
        jnp.bfloat16
    )


def local(
    forward_input,
    stored_input,
    output_gradient,
    frozen_weight,
    adapter_down_factor,
    adapter_up_factor,
    adapter_index_list,
):
    single_float = jnp.float32
    brain_half_float = jnp.bfloat16
    highest_accuracy = lax.Precision.HIGHEST
    owners_count = lax.axis_size("adapter")
    seq_count = adapter_index_list.shape[2]
    capacity = max(2, seq_count // owners_count + 1)
    slot_total = owners_count * capacity
    hidden_state = forward_input[0]
    saved = stored_input[0]
    cotangent = output_gradient[0]
    weight = frozen_weight[0]
    down_factor_table = adapter_down_factor[0]
    up_factor_table = adapter_up_factor[0]
    adapters_held = down_factor_table.shape[0]
    rows, width = hidden_state.shape
    seq_len = rows // seq_count
    forward_base_output = jnp.dot(
        lax.all_gather(hidden_state, "mp", axis=1, tiled=True),
        weight,
        preferred_element_type=single_float,
    )
    mp_count = lax.axis_size("mp")
    z_count = mp_count // Y_RING
    block = weight.shape[0] // mp_count
    half_rows = cotangent.shape[0] // 2
    weight_y_major = (
        weight.reshape(z_count, Y_RING, block, weight.shape[1])
        .transpose(1, 0, 2, 3)
        .reshape(weight.shape)
    )
    contract = (((1,), (1,)), ((), ()))
    back_z_major = lax.dot_general(
        cotangent[:half_rows], weight, contract, preferred_element_type=single_float
    ).astype(jnp.bfloat16)
    back_y_major = lax.dot_general(
        cotangent[half_rows:], weight_y_major, contract, preferred_element_type=single_float
    ).astype(jnp.bfloat16)
    base_back = torus_reduce_scatter(back_z_major, back_y_major, "adapter", "mp")
    forward_placement, pick_fwd = pack_slots(
        adapter_index_list[0, 0], capacity, owners_count, adapters_held
    )
    placing_back, pick_back = pack_slots(
        adapter_index_list[1, 0], capacity, owners_count, adapters_held
    )

    def to_slots(placing, values):
        flat_rows = values.reshape(seq_count, seq_len * width)
        packed = jnp.dot(placing, flat_rows, preferred_element_type=single_float).astype(
            brain_half_float
        )
        return packed.reshape(owners_count, capacity, seq_len, width)

    def slots_gathered(placing, values):
        flat_rows = values.reshape(slot_total, seq_len * width)
        spread = lax.dot_general(
            placing, flat_rows, (((0,), (0,)), ((), ())), preferred_element_type=single_float
        )
        return spread.reshape(rows, width)

    send_fwd = to_slots(forward_placement, hidden_state)
    send_saved = to_slots(placing_back, saved)
    send_grad = to_slots(placing_back, cotangent)
    rows_fwd = lax.all_to_all(send_fwd, "adapter", split_axis=0, concat_axis=0, tiled=True)
    rows_saved = lax.all_to_all(send_saved, "adapter", split_axis=0, concat_axis=0, tiled=True)
    token_row_gradient = lax.all_to_all(
        send_grad, "adapter", split_axis=0, concat_axis=0, tiled=True
    )
    owner_fwd = lax.all_to_all(pick_fwd, "adapter", split_axis=0, concat_axis=0, tiled=True)
    owner_back = lax.all_to_all(pick_back, "adapter", split_axis=0, concat_axis=0, tiled=True)
    first_fwd = select_slabs(owner_fwd, down_factor_table)
    second_fwd = select_slabs(owner_fwd, up_factor_table)
    first_back = select_slabs(owner_back, down_factor_table)
    second_back = select_slabs(owner_back, up_factor_table)
    rank_fwd = jnp.einsum(
        "nklm,nkrm->nkrl", rows_fwd, first_fwd, preferred_element_type=single_float
    )
    rank_back = jnp.einsum(
        "nklm,nkrm->nkrl", rows_saved, first_back, preferred_element_type=single_float
    )
    rank_space_gradient = jnp.einsum(
        "nklm,nkrm->nkrl", token_row_gradient, second_back, preferred_element_type=single_float
    )
    rank_fwd, rank_back, rank_space_gradient = halving_doubling_sum(
        (rank_fwd, rank_back, rank_space_gradient), "mp"
    )
    coded_fwd = rank_fwd.astype(brain_half_float)
    encoded_backward = rank_back.astype(brain_half_float)
    gradient_scaled = (adapter_scale * rank_space_gradient).astype(brain_half_float)
    adapter_token_rows = jnp.einsum(
        "nkrl,nkrm->nklm", coded_fwd, second_fwd, preferred_element_type=single_float
    ).astype(brain_half_float)
    back_rows = jnp.einsum(
        "nkrl,nkrm->nklm", gradient_scaled, first_back, preferred_element_type=single_float
    ).astype(brain_half_float)
    adapter_home_output = lax.all_to_all(
        adapter_token_rows, "adapter", split_axis=0, concat_axis=0, tiled=True
    )
    returned_home = lax.all_to_all(back_rows, "adapter", split_axis=0, concat_axis=0, tiled=True)
    slot_down_gradient = jnp.einsum(
        "nkrl,nklm->nkrm", gradient_scaled, rows_saved, preferred_element_type=single_float
    )
    slot_up_gradient = adapter_scale * jnp.einsum(
        "nkrl,nklm->nkrm", encoded_backward, token_row_gradient, preferred_element_type=single_float
    )
    adapter_home_output, returned_home, slot_down_gradient, slot_up_gradient, owner_selection = (
        adapter_home_output,
        returned_home,
        slot_down_gradient,
        slot_up_gradient,
        owner_back,
    )
    owner_weights = owner_selection.astype(single_float)
    grad_a = (
        jnp.einsum("nkj,nkrm->jrm", owner_weights, slot_down_gradient, precision=highest_accuracy)
        / seq_len
    ).astype(brain_half_float)
    grad_b = (
        jnp.einsum("nkj,nkrm->jrm", owner_weights, slot_up_gradient, precision=highest_accuracy)
        / seq_len
    ).astype(brain_half_float)
    adapter_sequence_output = slots_gathered(forward_placement, adapter_home_output)
    back_seq = slots_gathered(placing_back, returned_home)
    forward_output = (
        hidden_state.astype(single_float)
        + forward_base_output
        + adapter_scale * adapter_sequence_output
    ).astype(brain_half_float)
    out_back = (cotangent.astype(single_float) + base_back + back_seq).astype(brain_half_float)
    fwd_next = shifted(forward_output, "section", 1)
    back_next = shifted(out_back, "section", -1)
    return (fwd_next[None], back_next[None], grad_a[None], grad_b[None])


def solution(mesh):
    in_specs = (
        P("section", "adapter", "mp"),
        P("section", "adapter", "mp"),
        P("section", "adapter", "mp"),
        P("section", None, "mp"),
        P("section", "adapter", None, "mp"),
        P("section", "adapter", None, "mp"),
        P(None, "section", "adapter"),
    )
    out_specs = (
        P("section", "adapter", "mp"),
        P("section", "adapter", "mp"),
        P("section", "adapter", None, "mp"),
        P("section", "adapter", None, "mp"),
    )
    return jax.shard_map(local, mesh=mesh, in_specs=in_specs, out_specs=out_specs, check_vma=False)
```

```python
import jax
import jax.numpy as jnp
from jax import lax
from jax.sharding import PartitionSpec as P

adapter_scale = 2.0


def shifted(value, axis, steps):
    count = lax.axis_size(axis)
    pairs = [(source, (source + steps) % count) for source in range(count)]
    return lax.ppermute(value, axis, pairs)


def exchange(value, axis, bit):
    count = lax.axis_size(axis)
    pairs = [(source, source ^ (1 << bit)) for source in range(count)]
    return lax.ppermute(value, axis, pairs)


def halving_doubling_sum(values, axis):
    count = lax.axis_size(axis)
    levels = count.bit_length() - 1
    assert 1 << levels == count
    order = [0, 2, 1, 3, 4, 5, 6, 7, 8][:levels] if levels >= 3 else list(range(levels))
    order = [b for b in order if b < levels]
    me = lax.axis_index(axis)
    flat = jnp.concatenate([v.reshape(-1) for v in values])
    total = flat.shape[0]
    assert total % count == 0
    held = flat
    for bit in order:
        half = held.shape[0] // 2
        low, high = held[:half], held[half:]
        upper = ((me >> bit) & 1) == 1
        keep = jnp.where(upper, high, low)
        send = jnp.where(upper, low, high)
        held = keep + exchange(send, axis, bit)
    for bit in reversed(order):
        upper = ((me >> bit) & 1) == 1
        other = exchange(held, axis, bit)
        held = jnp.where(upper, jnp.concatenate([other, held]), jnp.concatenate([held, other]))
    pieces = []
    start = 0
    for v in values:
        pieces.append(held[start:start + v.size].reshape(v.shape))
        start += v.size
    return tuple(pieces)


Y_RING = 4


def ring_pairs(groups, count, z_step, y_step):
    z_count = count // Y_RING
    pairs = []
    for group in range(groups):
        sign = 1 if group % 2 == 0 else -1
        for source in range(count):
            z, y = divmod(source, Y_RING)
            target = ((z + sign * z_step) % z_count) * Y_RING + (y + sign * y_step) % Y_RING
            pairs.append((group * count + source, group * count + target))
    return pairs


def ring_reduce(partials, count, position, axes, pairs, sign):
    width = partials.shape[1] // count

    def own(offset):
        index = (position - sign * offset + 2 * count) % count
        return lax.dynamic_slice_in_dim(partials, index * width, width, axis=1).astype(
            jnp.float32
        )

    total = own(1)
    for step in range(1, count):
        arrived = lax.ppermute(total.astype(jnp.bfloat16), axes, pairs)
        total = arrived.astype(jnp.float32) + own(1 + step)
    return total


def torus_reduce_scatter(z_major, y_major, ring_axis, axis):
    count = lax.axis_size(axis)
    z_count = count // Y_RING
    groups = lax.axis_size(ring_axis)
    axes = (ring_axis, axis)
    sign = 1 - 2 * (lax.axis_index(ring_axis) % 2)
    me = lax.axis_index(axis)
    z_me, y_me = me // Y_RING, me % Y_RING
    z_pairs = ring_pairs(groups, count, 1, 0)
    y_pairs = ring_pairs(groups, count, 0, 1)
    along_z = ring_reduce(z_major, z_count, z_me, axes, z_pairs, sign)
    first = ring_reduce(along_z, Y_RING, y_me, axes, y_pairs, sign)
    along_y = ring_reduce(y_major, Y_RING, y_me, axes, y_pairs, sign)
    second = ring_reduce(along_y, z_count, z_me, axes, z_pairs, sign)
    return jnp.concatenate([first, second], axis=0)


def exchange_sum(values, axis):
    count = lax.axis_size(axis)
    flat = jnp.concatenate([v.reshape(-1) for v in values])
    assert flat.shape[0] % count == 0
    pieces = lax.all_to_all(flat.reshape(count, -1), axis, 0, 0, tiled=True)
    reduced = jnp.sum(pieces, axis=0)
    spread = jnp.broadcast_to(reduced[None], pieces.shape)
    held = lax.all_to_all(spread, axis, 0, 0, tiled=True).reshape(-1)
    out = []
    start = 0
    for v in values:
        out.append(held[start:start + v.size].reshape(v.shape))
        start += v.size
    return tuple(out)


def pack_slots(ids_row, capacity, owners_count, adapters_held):
    seq_count = ids_row.shape[0]
    owners = ids_row // adapters_held
    positions = jnp.arange(seq_count, dtype=jnp.int32)
    same_owner = owners[:, None] == owners[None, :]
    earlier = positions[None, :] < positions[:, None]
    slot_rank = jnp.sum((same_owner & earlier).astype(jnp.int32), axis=1)
    slot_index = owners * capacity + slot_rank
    slot_ids = jnp.arange(owners_count * capacity, dtype=jnp.int32)
    placing = (slot_index[None, :] == slot_ids[:, None]).astype(jnp.bfloat16)
    local_ids = ids_row % adapters_held
    pick_seq = (local_ids[:, None] == jnp.arange(adapters_held, dtype=jnp.int32)[None, :]).astype(
        jnp.bfloat16
    )
    chosen = jnp.dot(placing, pick_seq, preferred_element_type=jnp.float32).astype(jnp.bfloat16)
    return (placing, chosen.reshape(owners_count, capacity, adapters_held))


def select_slabs(chosen, table):
    return jnp.einsum("nkj,jrm->nkrm", chosen, table, preferred_element_type=jnp.float32).astype(
        jnp.bfloat16
    )


def local(
    forward_input,
    stored_input,
    output_gradient,
    frozen_weight,
    adapter_down_factor,
    adapter_up_factor,
    adapter_index_list,
):
    single_float = jnp.float32
    brain_half_float = jnp.bfloat16
    highest_accuracy = lax.Precision.HIGHEST
    owners_count = lax.axis_size("adapter")
    seq_count = adapter_index_list.shape[2]
    capacity = max(2, seq_count // owners_count + 1)
    slot_total = owners_count * capacity
    hidden_state = forward_input[0]
    saved = stored_input[0]
    cotangent = output_gradient[0]
    weight = frozen_weight[0]
    down_factor_table = adapter_down_factor[0]
    up_factor_table = adapter_up_factor[0]
    adapters_held = down_factor_table.shape[0]
    rows, width = hidden_state.shape
    seq_len = rows // seq_count
    forward_base_output = jnp.dot(
        lax.all_gather(hidden_state, "mp", axis=1, tiled=True),
        weight,
        preferred_element_type=single_float,
    )
    mp_count = lax.axis_size("mp")
    z_count = mp_count // Y_RING
    block = weight.shape[0] // mp_count
    half_rows = cotangent.shape[0] // 2
    weight_y_major = (
        weight.reshape(z_count, Y_RING, block, weight.shape[1])
        .transpose(1, 0, 2, 3)
        .reshape(weight.shape)
    )
    contract = (((1,), (1,)), ((), ()))
    back_z_major = lax.dot_general(
        cotangent[:half_rows], weight, contract, preferred_element_type=single_float
    ).astype(jnp.bfloat16)
    back_y_major = lax.dot_general(
        cotangent[half_rows:], weight_y_major, contract, preferred_element_type=single_float
    ).astype(jnp.bfloat16)
    base_back = torus_reduce_scatter(back_z_major, back_y_major, "adapter", "mp")
    forward_placement, pick_fwd = pack_slots(
        adapter_index_list[0, 0], capacity, owners_count, adapters_held
    )
    placing_back, pick_back = pack_slots(
        adapter_index_list[1, 0], capacity, owners_count, adapters_held
    )

    def to_slots(placing, values):
        flat_rows = values.reshape(seq_count, seq_len * width)
        packed = jnp.dot(placing, flat_rows, preferred_element_type=single_float).astype(
            brain_half_float
        )
        return packed.reshape(owners_count, capacity, seq_len, width)

    def slots_gathered(placing, values):
        flat_rows = values.reshape(slot_total, seq_len * width)
        spread = lax.dot_general(
            placing, flat_rows, (((0,), (0,)), ((), ())), preferred_element_type=single_float
        )
        return spread.reshape(rows, width)

    send_fwd = to_slots(forward_placement, hidden_state)
    send_saved = to_slots(placing_back, saved)
    send_grad = to_slots(placing_back, cotangent)
    rows_fwd = lax.all_to_all(send_fwd, "adapter", split_axis=0, concat_axis=0, tiled=True)
    rows_saved = lax.all_to_all(send_saved, "adapter", split_axis=0, concat_axis=0, tiled=True)
    token_row_gradient = lax.all_to_all(
        send_grad, "adapter", split_axis=0, concat_axis=0, tiled=True
    )
    owner_fwd = lax.all_to_all(pick_fwd, "adapter", split_axis=0, concat_axis=0, tiled=True)
    owner_back = lax.all_to_all(pick_back, "adapter", split_axis=0, concat_axis=0, tiled=True)
    first_fwd = select_slabs(owner_fwd, down_factor_table)
    second_fwd = select_slabs(owner_fwd, up_factor_table)
    first_back = select_slabs(owner_back, down_factor_table)
    second_back = select_slabs(owner_back, up_factor_table)
    rank_fwd = jnp.einsum(
        "nklm,nkrm->nkrl", rows_fwd, first_fwd, preferred_element_type=single_float
    )
    rank_back = jnp.einsum(
        "nklm,nkrm->nkrl", rows_saved, first_back, preferred_element_type=single_float
    )
    rank_space_gradient = jnp.einsum(
        "nklm,nkrm->nkrl", token_row_gradient, second_back, preferred_element_type=single_float
    )
    rank_fwd, rank_back, rank_space_gradient = exchange_sum(
        (rank_fwd, rank_back, rank_space_gradient), "mp"
    )
    coded_fwd = rank_fwd.astype(brain_half_float)
    encoded_backward = rank_back.astype(brain_half_float)
    gradient_scaled = (adapter_scale * rank_space_gradient).astype(brain_half_float)
    adapter_token_rows = jnp.einsum(
        "nkrl,nkrm->nklm", coded_fwd, second_fwd, preferred_element_type=single_float
    ).astype(brain_half_float)
    back_rows = jnp.einsum(
        "nkrl,nkrm->nklm", gradient_scaled, first_back, preferred_element_type=single_float
    ).astype(brain_half_float)
    adapter_home_output = lax.all_to_all(
        adapter_token_rows, "adapter", split_axis=0, concat_axis=0, tiled=True
    )
    returned_home = lax.all_to_all(back_rows, "adapter", split_axis=0, concat_axis=0, tiled=True)
    slot_down_gradient = jnp.einsum(
        "nkrl,nklm->nkrm", gradient_scaled, rows_saved, preferred_element_type=single_float
    )
    slot_up_gradient = adapter_scale * jnp.einsum(
        "nkrl,nklm->nkrm", encoded_backward, token_row_gradient, preferred_element_type=single_float
    )
    adapter_home_output, returned_home, slot_down_gradient, slot_up_gradient, owner_selection = (
        adapter_home_output,
        returned_home,
        slot_down_gradient,
        slot_up_gradient,
        owner_back,
    )
    owner_weights = owner_selection.astype(single_float)
    grad_a = (
        jnp.einsum("nkj,nkrm->jrm", owner_weights, slot_down_gradient, precision=highest_accuracy)
        / seq_len
    ).astype(brain_half_float)
    grad_b = (
        jnp.einsum("nkj,nkrm->jrm", owner_weights, slot_up_gradient, precision=highest_accuracy)
        / seq_len
    ).astype(brain_half_float)
    adapter_sequence_output = slots_gathered(forward_placement, adapter_home_output)
    back_seq = slots_gathered(placing_back, returned_home)
    forward_output = (
        hidden_state.astype(single_float)
        + forward_base_output
        + adapter_scale * adapter_sequence_output
    ).astype(brain_half_float)
    out_back = (cotangent.astype(single_float) + base_back + back_seq).astype(brain_half_float)
    fwd_next = shifted(forward_output, "section", 1)
    back_next = shifted(out_back, "section", -1)
    return (fwd_next[None], back_next[None], grad_a[None], grad_b[None])


def solution(mesh):
    in_specs = (
        P("section", "adapter", "mp"),
        P("section", "adapter", "mp"),
        P("section", "adapter", "mp"),
        P("section", None, "mp"),
        P("section", "adapter", None, "mp"),
        P("section", "adapter", None, "mp"),
        P(None, "section", "adapter"),
    )
    out_specs = (
        P("section", "adapter", "mp"),
        P("section", "adapter", "mp"),
        P("section", "adapter", None, "mp"),
        P("section", "adapter", None, "mp"),
    )
    return jax.shard_map(local, mesh=mesh, in_specs=in_specs, out_specs=out_specs, check_vma=False)
```

```python
import jax
import jax.numpy as jnp
from jax import lax
from jax.sharding import PartitionSpec as P

adapter_scale = 2.0


def shifted(value, axis, steps):
    count = lax.axis_size(axis)
    pairs = [(source, (source + steps) % count) for source in range(count)]
    return lax.ppermute(value, axis, pairs)


def exchange(value, axis, bit):
    count = lax.axis_size(axis)
    pairs = [(source, source ^ (1 << bit)) for source in range(count)]
    return lax.ppermute(value, axis, pairs)


def halving_doubling_sum(values, axis):
    count = lax.axis_size(axis)
    levels = count.bit_length() - 1
    assert 1 << levels == count
    order = [0, 2, 1, 3, 4, 5, 6, 7, 8][:levels] if levels >= 3 else list(range(levels))
    order = [b for b in order if b < levels]
    me = lax.axis_index(axis)
    flat = jnp.concatenate([v.reshape(-1) for v in values])
    total = flat.shape[0]
    assert total % count == 0
    held = flat
    for bit in order:
        half = held.shape[0] // 2
        low, high = held[:half], held[half:]
        upper = ((me >> bit) & 1) == 1
        keep = jnp.where(upper, high, low)
        send = jnp.where(upper, low, high)
        held = keep + exchange(send, axis, bit)
    for bit in reversed(order):
        upper = ((me >> bit) & 1) == 1
        other = exchange(held, axis, bit)
        held = jnp.where(upper, jnp.concatenate([other, held]), jnp.concatenate([held, other]))
    pieces = []
    start = 0
    for v in values:
        pieces.append(held[start:start + v.size].reshape(v.shape))
        start += v.size
    return tuple(pieces)


Y_RING = 4


def ring_pairs(groups, count, z_step, y_step):
    z_count = count // Y_RING
    pairs = []
    for group in range(groups):
        sign = 1 if group % 2 == 0 else -1
        for source in range(count):
            z, y = divmod(source, Y_RING)
            target = ((z + sign * z_step) % z_count) * Y_RING + (y + sign * y_step) % Y_RING
            pairs.append((group * count + source, group * count + target))
    return pairs


def ring_reduce(partials, count, position, axes, pairs, sign, gate=None):
    width = partials.shape[1] // count

    def own(offset):
        index = (position - sign * offset + 2 * count) % count
        return lax.dynamic_slice_in_dim(partials, index * width, width, axis=1).astype(
            jnp.float32
        )

    total = own(1)
    for step in range(1, count):
        if gate is not None and step == count - 1:
            total, gate = lax.optimization_barrier((total, gate))
        arrived = lax.ppermute(total.astype(jnp.bfloat16), axes, pairs)
        total = arrived.astype(jnp.float32) + own(1 + step)
    return total


def torus_reduce_scatter(z_major, y_major, ring_axis, axis, gate=None):
    count = lax.axis_size(axis)
    z_count = count // Y_RING
    groups = lax.axis_size(ring_axis)
    axes = (ring_axis, axis)
    sign = 1 - 2 * (lax.axis_index(ring_axis) % 2)
    me = lax.axis_index(axis)
    z_me, y_me = me // Y_RING, me % Y_RING
    z_pairs = ring_pairs(groups, count, 1, 0)
    y_pairs = ring_pairs(groups, count, 0, 1)
    along_z = ring_reduce(z_major, z_count, z_me, axes, z_pairs, sign)
    first = ring_reduce(along_z, Y_RING, y_me, axes, y_pairs, sign, gate)
    along_y = ring_reduce(y_major, Y_RING, y_me, axes, y_pairs, sign)
    second = ring_reduce(along_y, z_count, z_me, axes, z_pairs, sign, gate)
    return jnp.concatenate([first, second], axis=0)


def exchange_sum(values, axis):
    count = lax.axis_size(axis)
    flat = jnp.concatenate([v.reshape(-1) for v in values])
    assert flat.shape[0] % count == 0
    pieces = lax.all_to_all(flat.reshape(count, -1), axis, 0, 0, tiled=True)
    reduced = jnp.sum(pieces, axis=0)
    spread = jnp.broadcast_to(reduced[None], pieces.shape)
    held = lax.all_to_all(spread, axis, 0, 0, tiled=True).reshape(-1)
    out = []
    start = 0
    for v in values:
        out.append(held[start:start + v.size].reshape(v.shape))
        start += v.size
    return tuple(out)


def pack_slots(ids_row, capacity, owners_count, adapters_held):
    seq_count = ids_row.shape[0]
    owners = ids_row // adapters_held
    positions = jnp.arange(seq_count, dtype=jnp.int32)
    same_owner = owners[:, None] == owners[None, :]
    earlier = positions[None, :] < positions[:, None]
    slot_rank = jnp.sum((same_owner & earlier).astype(jnp.int32), axis=1)
    slot_index = owners * capacity + slot_rank
    slot_ids = jnp.arange(owners_count * capacity, dtype=jnp.int32)
    placing = (slot_index[None, :] == slot_ids[:, None]).astype(jnp.bfloat16)
    local_ids = ids_row % adapters_held
    pick_seq = (local_ids[:, None] == jnp.arange(adapters_held, dtype=jnp.int32)[None, :]).astype(
        jnp.bfloat16
    )
    chosen = jnp.dot(placing, pick_seq, preferred_element_type=jnp.float32).astype(jnp.bfloat16)
    return (placing, chosen.reshape(owners_count, capacity, adapters_held))


def select_slabs(chosen, table):
    return jnp.einsum("nkj,jrm->nkrm", chosen, table, preferred_element_type=jnp.float32).astype(
        jnp.bfloat16
    )


def local(
    forward_input,
    stored_input,
    output_gradient,
    frozen_weight,
    adapter_down_factor,
    adapter_up_factor,
    adapter_index_list,
):
    single_float = jnp.float32
    brain_half_float = jnp.bfloat16
    highest_accuracy = lax.Precision.HIGHEST
    owners_count = lax.axis_size("adapter")
    seq_count = adapter_index_list.shape[2]
    capacity = max(2, seq_count // owners_count + 1)
    slot_total = owners_count * capacity
    hidden_state = forward_input[0]
    saved = stored_input[0]
    cotangent = output_gradient[0]
    weight = frozen_weight[0]
    down_factor_table = adapter_down_factor[0]
    up_factor_table = adapter_up_factor[0]
    adapters_held = down_factor_table.shape[0]
    rows, width = hidden_state.shape
    seq_len = rows // seq_count
    forward_base_output = jnp.dot(
        lax.all_gather(hidden_state, "mp", axis=1, tiled=True),
        weight,
        preferred_element_type=single_float,
    )
    mp_count = lax.axis_size("mp")
    z_count = mp_count // Y_RING
    block = weight.shape[0] // mp_count
    half_rows = cotangent.shape[0] // 2
    weight_y_major = (
        weight.reshape(z_count, Y_RING, block, weight.shape[1])
        .transpose(1, 0, 2, 3)
        .reshape(weight.shape)
    )
    contract = (((1,), (1,)), ((), ()))
    back_z_major = lax.dot_general(
        cotangent[:half_rows], weight, contract, preferred_element_type=single_float
    ).astype(jnp.bfloat16)
    back_y_major = lax.dot_general(
        cotangent[half_rows:], weight_y_major, contract, preferred_element_type=single_float
    ).astype(jnp.bfloat16)
    forward_placement, pick_fwd = pack_slots(
        adapter_index_list[0, 0], capacity, owners_count, adapters_held
    )
    placing_back, pick_back = pack_slots(
        adapter_index_list[1, 0], capacity, owners_count, adapters_held
    )

    def to_slots(placing, values):
        flat_rows = values.reshape(seq_count, seq_len * width)
        packed = jnp.dot(placing, flat_rows, preferred_element_type=single_float).astype(
            brain_half_float
        )
        return packed.reshape(owners_count, capacity, seq_len, width)

    def slots_gathered(placing, values):
        flat_rows = values.reshape(slot_total, seq_len * width)
        spread = lax.dot_general(
            placing, flat_rows, (((0,), (0,)), ((), ())), preferred_element_type=single_float
        )
        return spread.reshape(rows, width)

    send_fwd = to_slots(forward_placement, hidden_state)
    send_saved = to_slots(placing_back, saved)
    send_grad = to_slots(placing_back, cotangent)
    rows_fwd = lax.all_to_all(send_fwd, "adapter", split_axis=0, concat_axis=0, tiled=True)
    rows_saved = lax.all_to_all(send_saved, "adapter", split_axis=0, concat_axis=0, tiled=True)
    token_row_gradient = lax.all_to_all(
        send_grad, "adapter", split_axis=0, concat_axis=0, tiled=True
    )
    owner_fwd = lax.all_to_all(pick_fwd, "adapter", split_axis=0, concat_axis=0, tiled=True)
    owner_back = lax.all_to_all(pick_back, "adapter", split_axis=0, concat_axis=0, tiled=True)
    first_fwd = select_slabs(owner_fwd, down_factor_table)
    second_fwd = select_slabs(owner_fwd, up_factor_table)
    first_back = select_slabs(owner_back, down_factor_table)
    second_back = select_slabs(owner_back, up_factor_table)
    rank_fwd = jnp.einsum(
        "nklm,nkrm->nkrl", rows_fwd, first_fwd, preferred_element_type=single_float
    )
    rank_back = jnp.einsum(
        "nklm,nkrm->nkrl", rows_saved, first_back, preferred_element_type=single_float
    )
    rank_space_gradient = jnp.einsum(
        "nklm,nkrm->nkrl", token_row_gradient, second_back, preferred_element_type=single_float
    )
    rank_fwd, rank_back, rank_space_gradient = exchange_sum(
        (rank_fwd, rank_back, rank_space_gradient), "mp"
    )
    coded_fwd = rank_fwd.astype(brain_half_float)
    encoded_backward = rank_back.astype(brain_half_float)
    gradient_scaled = (adapter_scale * rank_space_gradient).astype(brain_half_float)
    adapter_token_rows = jnp.einsum(
        "nkrl,nkrm->nklm", coded_fwd, second_fwd, preferred_element_type=single_float
    ).astype(brain_half_float)
    back_rows = jnp.einsum(
        "nkrl,nkrm->nklm", gradient_scaled, first_back, preferred_element_type=single_float
    ).astype(brain_half_float)
    adapter_home_output = lax.all_to_all(
        adapter_token_rows, "adapter", split_axis=0, concat_axis=0, tiled=True
    )
    returned_home = lax.all_to_all(back_rows, "adapter", split_axis=0, concat_axis=0, tiled=True)
    slot_down_gradient = jnp.einsum(
        "nkrl,nklm->nkrm", gradient_scaled, rows_saved, preferred_element_type=single_float
    )
    slot_up_gradient = adapter_scale * jnp.einsum(
        "nkrl,nklm->nkrm", encoded_backward, token_row_gradient, preferred_element_type=single_float
    )
    adapter_home_output, returned_home, slot_down_gradient, slot_up_gradient, owner_selection = (
        adapter_home_output,
        returned_home,
        slot_down_gradient,
        slot_up_gradient,
        owner_back,
    )
    owner_weights = owner_selection.astype(single_float)
    grad_a = (
        jnp.einsum("nkj,nkrm->jrm", owner_weights, slot_down_gradient, precision=highest_accuracy)
        / seq_len
    ).astype(brain_half_float)
    grad_b = (
        jnp.einsum("nkj,nkrm->jrm", owner_weights, slot_up_gradient, precision=highest_accuracy)
        / seq_len
    ).astype(brain_half_float)
    adapter_sequence_output = slots_gathered(forward_placement, adapter_home_output)
    back_seq = slots_gathered(placing_back, returned_home)
    forward_output = (
        hidden_state.astype(single_float)
        + forward_base_output
        + adapter_scale * adapter_sequence_output
    ).astype(brain_half_float)
    base_back = torus_reduce_scatter(
        back_z_major, back_y_major, "adapter", "mp", gate=forward_output
    )
    out_back = (cotangent.astype(single_float) + base_back + back_seq).astype(brain_half_float)
    fwd_next = shifted(forward_output, "section", 1)
    back_next = shifted(out_back, "section", -1)
    return (fwd_next[None], back_next[None], grad_a[None], grad_b[None])


def solution(mesh):
    in_specs = (
        P("section", "adapter", "mp"),
        P("section", "adapter", "mp"),
        P("section", "adapter", "mp"),
        P("section", None, "mp"),
        P("section", "adapter", None, "mp"),
        P("section", "adapter", None, "mp"),
        P(None, "section", "adapter"),
    )
    out_specs = (
        P("section", "adapter", "mp"),
        P("section", "adapter", "mp"),
        P("section", "adapter", None, "mp"),
        P("section", "adapter", None, "mp"),
    )
    return jax.shard_map(local, mesh=mesh, in_specs=in_specs, out_specs=out_specs, check_vma=False)
```

```python
import jax
import jax.numpy as jnp
from jax import lax
from jax.sharding import PartitionSpec as P

adapter_scale = 2.0


def shifted(value, axis, steps):
    count = lax.axis_size(axis)
    pairs = [(source, (source + steps) % count) for source in range(count)]
    return lax.ppermute(value, axis, pairs)


def exchange(value, axis, bit):
    count = lax.axis_size(axis)
    pairs = [(source, source ^ (1 << bit)) for source in range(count)]
    return lax.ppermute(value, axis, pairs)


def halving_doubling_sum(values, axis):
    count = lax.axis_size(axis)
    levels = count.bit_length() - 1
    assert 1 << levels == count
    order = [0, 2, 1, 3, 4, 5, 6, 7, 8][:levels] if levels >= 3 else list(range(levels))
    order = [b for b in order if b < levels]
    me = lax.axis_index(axis)
    flat = jnp.concatenate([v.reshape(-1) for v in values])
    total = flat.shape[0]
    assert total % count == 0
    held = flat
    for bit in order:
        half = held.shape[0] // 2
        low, high = held[:half], held[half:]
        upper = ((me >> bit) & 1) == 1
        keep = jnp.where(upper, high, low)
        send = jnp.where(upper, low, high)
        held = keep + exchange(send, axis, bit)
    for bit in reversed(order):
        upper = ((me >> bit) & 1) == 1
        other = exchange(held, axis, bit)
        held = jnp.where(upper, jnp.concatenate([other, held]), jnp.concatenate([held, other]))
    pieces = []
    start = 0
    for v in values:
        pieces.append(held[start:start + v.size].reshape(v.shape))
        start += v.size
    return tuple(pieces)


Y_RING = 4


def ring_pairs(groups, count, z_step, y_step):
    z_count = count // Y_RING
    pairs = []
    for group in range(groups):
        sign = 1 if group % 2 == 0 else -1
        for source in range(count):
            z, y = divmod(source, Y_RING)
            target = ((z + sign * z_step) % z_count) * Y_RING + (y + sign * y_step) % Y_RING
            pairs.append((group * count + source, group * count + target))
    return pairs


def ring_reduce(partials, count, position, axes, pairs, sign):
    width = partials.shape[1] // count

    def own(offset):
        index = (position - sign * offset + 2 * count) % count
        return lax.dynamic_slice_in_dim(partials, index * width, width, axis=1).astype(
            jnp.float32
        )

    total = own(1)
    for step in range(1, count):
        arrived = lax.ppermute(total.astype(jnp.bfloat16), axes, pairs)
        total = arrived.astype(jnp.float32) + own(1 + step)
    return total


def torus_reduce_scatter(z_major, y_major, ring_axis, axis):
    count = lax.axis_size(axis)
    z_count = count // Y_RING
    groups = lax.axis_size(ring_axis)
    axes = (ring_axis, axis)
    sign = 1 - 2 * (lax.axis_index(ring_axis) % 2)
    me = lax.axis_index(axis)
    z_me, y_me = me // Y_RING, me % Y_RING
    z_pairs = ring_pairs(groups, count, 1, 0)
    y_pairs = ring_pairs(groups, count, 0, 1)
    along_z = ring_reduce(z_major, z_count, z_me, axes, z_pairs, sign)
    first = ring_reduce(along_z, Y_RING, y_me, axes, y_pairs, sign)
    along_y = ring_reduce(y_major, Y_RING, y_me, axes, y_pairs, sign)
    second = ring_reduce(along_y, z_count, z_me, axes, z_pairs, sign)
    return jnp.concatenate([first, second], axis=0)


def exchange_sum(values, axis):
    count = lax.axis_size(axis)
    flat = jnp.concatenate([v.reshape(-1) for v in values])
    assert flat.shape[0] % count == 0
    pieces = lax.all_to_all(flat.reshape(count, -1), axis, 0, 0, tiled=True)
    reduced = jnp.sum(pieces, axis=0)
    spread = jnp.broadcast_to(reduced[None], pieces.shape)
    held = lax.all_to_all(spread, axis, 0, 0, tiled=True).reshape(-1)
    out = []
    start = 0
    for v in values:
        out.append(held[start:start + v.size].reshape(v.shape))
        start += v.size
    return tuple(out)


def pack_slots(ids_row, capacity, owners_count, adapters_held):
    seq_count = ids_row.shape[0]
    owners = ids_row // adapters_held
    positions = jnp.arange(seq_count, dtype=jnp.int32)
    same_owner = owners[:, None] == owners[None, :]
    earlier = positions[None, :] < positions[:, None]
    slot_rank = jnp.sum((same_owner & earlier).astype(jnp.int32), axis=1)
    slot_index = owners * capacity + slot_rank
    slot_ids = jnp.arange(owners_count * capacity, dtype=jnp.int32)
    placing = (slot_index[None, :] == slot_ids[:, None]).astype(jnp.bfloat16)
    local_ids = ids_row % adapters_held
    pick_seq = (local_ids[:, None] == jnp.arange(adapters_held, dtype=jnp.int32)[None, :]).astype(
        jnp.bfloat16
    )
    chosen = jnp.dot(placing, pick_seq, preferred_element_type=jnp.float32).astype(jnp.bfloat16)
    return (placing, chosen.reshape(owners_count, capacity, adapters_held))


def select_slabs(chosen, table):
    return jnp.einsum("nkj,jrm->nkrm", chosen, table, preferred_element_type=jnp.float32).astype(
        jnp.bfloat16
    )


def local(
    forward_input,
    stored_input,
    output_gradient,
    frozen_weight,
    adapter_down_factor,
    adapter_up_factor,
    adapter_index_list,
):
    single_float = jnp.float32
    brain_half_float = jnp.bfloat16
    highest_accuracy = lax.Precision.HIGHEST
    owners_count = lax.axis_size("adapter")
    seq_count = adapter_index_list.shape[2]
    capacity = max(2, seq_count // owners_count + 1)
    slot_total = owners_count * capacity
    hidden_state = forward_input[0]
    saved = stored_input[0]
    cotangent = output_gradient[0]
    weight = frozen_weight[0]
    down_factor_table = adapter_down_factor[0]
    up_factor_table = adapter_up_factor[0]
    adapters_held = down_factor_table.shape[0]
    rows, width = hidden_state.shape
    seq_len = rows // seq_count
    forward_base_output = jnp.dot(
        lax.all_gather(hidden_state, "mp", axis=1, tiled=True),
        weight,
        preferred_element_type=single_float,
    )
    mp_count = lax.axis_size("mp")
    z_count = mp_count // Y_RING
    block = weight.shape[0] // mp_count
    queued_rows = cotangent.shape[0] // 4
    half_rows = (cotangent.shape[0] - queued_rows) // 2
    weight_y_major = (
        weight.reshape(z_count, Y_RING, block, weight.shape[1])
        .transpose(1, 0, 2, 3)
        .reshape(weight.shape)
    )
    contract = (((1,), (1,)), ((), ()))
    back_queued = lax.dot_general(
        cotangent[:queued_rows], weight, contract, preferred_element_type=single_float
    ).astype(jnp.bfloat16)
    back_z_major = lax.dot_general(
        cotangent[queued_rows:queued_rows + half_rows],
        weight,
        contract,
        preferred_element_type=single_float,
    ).astype(jnp.bfloat16)
    back_y_major = lax.dot_general(
        cotangent[queued_rows + half_rows:],
        weight_y_major,
        contract,
        preferred_element_type=single_float,
    ).astype(jnp.bfloat16)
    base_back = jnp.concatenate(
        [
            lax.psum_scatter(back_queued, "mp", scatter_dimension=1, tiled=True).astype(
                single_float
            ),
            torus_reduce_scatter(back_z_major, back_y_major, "adapter", "mp"),
        ],
        axis=0,
    )
    forward_placement, pick_fwd = pack_slots(
        adapter_index_list[0, 0], capacity, owners_count, adapters_held
    )
    placing_back, pick_back = pack_slots(
        adapter_index_list[1, 0], capacity, owners_count, adapters_held
    )

    def to_slots(placing, values):
        flat_rows = values.reshape(seq_count, seq_len * width)
        packed = jnp.dot(placing, flat_rows, preferred_element_type=single_float).astype(
            brain_half_float
        )
        return packed.reshape(owners_count, capacity, seq_len, width)

    def slots_gathered(placing, values):
        flat_rows = values.reshape(slot_total, seq_len * width)
        spread = lax.dot_general(
            placing, flat_rows, (((0,), (0,)), ((), ())), preferred_element_type=single_float
        )
        return spread.reshape(rows, width)

    send_fwd = to_slots(forward_placement, hidden_state)
    send_saved = to_slots(placing_back, saved)
    send_grad = to_slots(placing_back, cotangent)
    rows_fwd = lax.all_to_all(send_fwd, "adapter", split_axis=0, concat_axis=0, tiled=True)
    rows_saved = lax.all_to_all(send_saved, "adapter", split_axis=0, concat_axis=0, tiled=True)
    token_row_gradient = lax.all_to_all(
        send_grad, "adapter", split_axis=0, concat_axis=0, tiled=True
    )
    owner_fwd = lax.all_to_all(pick_fwd, "adapter", split_axis=0, concat_axis=0, tiled=True)
    owner_back = lax.all_to_all(pick_back, "adapter", split_axis=0, concat_axis=0, tiled=True)
    first_fwd = select_slabs(owner_fwd, down_factor_table)
    second_fwd = select_slabs(owner_fwd, up_factor_table)
    first_back = select_slabs(owner_back, down_factor_table)
    second_back = select_slabs(owner_back, up_factor_table)
    rank_fwd = jnp.einsum(
        "nklm,nkrm->nkrl", rows_fwd, first_fwd, preferred_element_type=single_float
    )
    rank_back = jnp.einsum(
        "nklm,nkrm->nkrl", rows_saved, first_back, preferred_element_type=single_float
    )
    rank_space_gradient = jnp.einsum(
        "nklm,nkrm->nkrl", token_row_gradient, second_back, preferred_element_type=single_float
    )
    rank_fwd, rank_back, rank_space_gradient = exchange_sum(
        (rank_fwd, rank_back, rank_space_gradient), "mp"
    )
    coded_fwd = rank_fwd.astype(brain_half_float)
    encoded_backward = rank_back.astype(brain_half_float)
    gradient_scaled = (adapter_scale * rank_space_gradient).astype(brain_half_float)
    adapter_token_rows = jnp.einsum(
        "nkrl,nkrm->nklm", coded_fwd, second_fwd, preferred_element_type=single_float
    ).astype(brain_half_float)
    back_rows = jnp.einsum(
        "nkrl,nkrm->nklm", gradient_scaled, first_back, preferred_element_type=single_float
    ).astype(brain_half_float)
    adapter_home_output = lax.all_to_all(
        adapter_token_rows, "adapter", split_axis=0, concat_axis=0, tiled=True
    )
    returned_home = lax.all_to_all(back_rows, "adapter", split_axis=0, concat_axis=0, tiled=True)
    slot_down_gradient = jnp.einsum(
        "nkrl,nklm->nkrm", gradient_scaled, rows_saved, preferred_element_type=single_float
    )
    slot_up_gradient = adapter_scale * jnp.einsum(
        "nkrl,nklm->nkrm", encoded_backward, token_row_gradient, preferred_element_type=single_float
    )
    adapter_home_output, returned_home, slot_down_gradient, slot_up_gradient, owner_selection = (
        adapter_home_output,
        returned_home,
        slot_down_gradient,
        slot_up_gradient,
        owner_back,
    )
    owner_weights = owner_selection.astype(single_float)
    grad_a = (
        jnp.einsum("nkj,nkrm->jrm", owner_weights, slot_down_gradient, precision=highest_accuracy)
        / seq_len
    ).astype(brain_half_float)
    grad_b = (
        jnp.einsum("nkj,nkrm->jrm", owner_weights, slot_up_gradient, precision=highest_accuracy)
        / seq_len
    ).astype(brain_half_float)
    adapter_sequence_output = slots_gathered(forward_placement, adapter_home_output)
    back_seq = slots_gathered(placing_back, returned_home)
    forward_output = (
        hidden_state.astype(single_float)
        + forward_base_output
        + adapter_scale * adapter_sequence_output
    ).astype(brain_half_float)
    out_back = (cotangent.astype(single_float) + base_back + back_seq).astype(brain_half_float)
    fwd_next = shifted(forward_output, "section", 1)
    back_next = shifted(out_back, "section", -1)
    return (fwd_next[None], back_next[None], grad_a[None], grad_b[None])


def solution(mesh):
    in_specs = (
        P("section", "adapter", "mp"),
        P("section", "adapter", "mp"),
        P("section", "adapter", "mp"),
        P("section", None, "mp"),
        P("section", "adapter", None, "mp"),
        P("section", "adapter", None, "mp"),
        P(None, "section", "adapter"),
    )
    out_specs = (
        P("section", "adapter", "mp"),
        P("section", "adapter", "mp"),
        P("section", "adapter", None, "mp"),
        P("section", "adapter", None, "mp"),
    )
    return jax.shard_map(local, mesh=mesh, in_specs=in_specs, out_specs=out_specs, check_vma=False)
```

```python
import jax
import jax.numpy as jnp
from jax import lax
from jax.sharding import PartitionSpec as P

adapter_scale = 2.0


def shifted(value, axis, steps):
    count = lax.axis_size(axis)
    pairs = [(source, (source + steps) % count) for source in range(count)]
    return lax.ppermute(value, axis, pairs)


def exchange(value, axis, bit):
    count = lax.axis_size(axis)
    pairs = [(source, source ^ (1 << bit)) for source in range(count)]
    return lax.ppermute(value, axis, pairs)


def halving_doubling_sum(values, axis):
    count = lax.axis_size(axis)
    levels = count.bit_length() - 1
    assert 1 << levels == count
    order = [0, 2, 1, 3, 4, 5, 6, 7, 8][:levels] if levels >= 3 else list(range(levels))
    order = [b for b in order if b < levels]
    me = lax.axis_index(axis)
    flat = jnp.concatenate([v.reshape(-1) for v in values])
    total = flat.shape[0]
    assert total % count == 0
    held = flat
    for bit in order:
        half = held.shape[0] // 2
        low, high = held[:half], held[half:]
        upper = ((me >> bit) & 1) == 1
        keep = jnp.where(upper, high, low)
        send = jnp.where(upper, low, high)
        held = keep + exchange(send, axis, bit)
    for bit in reversed(order):
        upper = ((me >> bit) & 1) == 1
        other = exchange(held, axis, bit)
        held = jnp.where(upper, jnp.concatenate([other, held]), jnp.concatenate([held, other]))
    pieces = []
    start = 0
    for v in values:
        pieces.append(held[start:start + v.size].reshape(v.shape))
        start += v.size
    return tuple(pieces)


Y_RING = 4


def ring_pairs(groups, count, z_step, y_step):
    z_count = count // Y_RING
    pairs = []
    for group in range(groups):
        sign = 1 if group % 2 == 0 else -1
        for source in range(count):
            z, y = divmod(source, Y_RING)
            target = ((z + sign * z_step) % z_count) * Y_RING + (y + sign * y_step) % Y_RING
            pairs.append((group * count + source, group * count + target))
    return pairs


def ring_reduce(partials, count, position, axes, pairs, sign):
    width = partials.shape[1] // count

    def own(offset):
        index = (position - sign * offset + 2 * count) % count
        return lax.dynamic_slice_in_dim(partials, index * width, width, axis=1).astype(
            jnp.float32
        )

    total = own(1)
    for step in range(1, count):
        arrived = lax.ppermute(total.astype(jnp.bfloat16), axes, pairs)
        total = arrived.astype(jnp.float32) + own(1 + step)
    return total


def torus_reduce_scatter(z_major, y_major, ring_axis, axis):
    count = lax.axis_size(axis)
    z_count = count // Y_RING
    groups = lax.axis_size(ring_axis)
    axes = (ring_axis, axis)
    sign = 1 - 2 * (lax.axis_index(ring_axis) % 2)
    me = lax.axis_index(axis)
    z_me, y_me = me // Y_RING, me % Y_RING
    z_pairs = ring_pairs(groups, count, 1, 0)
    y_pairs = ring_pairs(groups, count, 0, 1)
    along_z = ring_reduce(z_major, z_count, z_me, axes, z_pairs, sign)
    first = ring_reduce(along_z, Y_RING, y_me, axes, y_pairs, sign)
    along_y = ring_reduce(y_major, Y_RING, y_me, axes, y_pairs, sign)
    second = ring_reduce(along_y, z_count, z_me, axes, z_pairs, sign)
    return jnp.concatenate([first, second], axis=0)


def exchange_sum(values, axis):
    count = lax.axis_size(axis)
    flat = jnp.concatenate([v.reshape(-1) for v in values])
    assert flat.shape[0] % count == 0
    pieces = lax.all_to_all(flat.reshape(count, -1), axis, 0, 0, tiled=True)
    reduced = jnp.sum(pieces, axis=0)
    spread = jnp.broadcast_to(reduced[None], pieces.shape)
    held = lax.all_to_all(spread, axis, 0, 0, tiled=True).reshape(-1)
    out = []
    start = 0
    for v in values:
        out.append(held[start:start + v.size].reshape(v.shape))
        start += v.size
    return tuple(out)


def pack_slots(ids_row, capacity, owners_count, adapters_held):
    seq_count = ids_row.shape[0]
    owners = ids_row // adapters_held
    positions = jnp.arange(seq_count, dtype=jnp.int32)
    same_owner = owners[:, None] == owners[None, :]
    earlier = positions[None, :] < positions[:, None]
    slot_rank = jnp.sum((same_owner & earlier).astype(jnp.int32), axis=1)
    slot_index = owners * capacity + slot_rank
    slot_ids = jnp.arange(owners_count * capacity, dtype=jnp.int32)
    placing = (slot_index[None, :] == slot_ids[:, None]).astype(jnp.bfloat16)
    local_ids = ids_row % adapters_held
    pick_seq = (local_ids[:, None] == jnp.arange(adapters_held, dtype=jnp.int32)[None, :]).astype(
        jnp.bfloat16
    )
    chosen = jnp.dot(placing, pick_seq, preferred_element_type=jnp.float32).astype(jnp.bfloat16)
    return (placing, chosen.reshape(owners_count, capacity, adapters_held))


def select_slabs(chosen, table):
    return jnp.einsum("nkj,jrm->nkrm", chosen, table, preferred_element_type=jnp.float32).astype(
        jnp.bfloat16
    )


def local(
    forward_input,
    stored_input,
    output_gradient,
    frozen_weight,
    adapter_down_factor,
    adapter_up_factor,
    adapter_index_list,
):
    single_float = jnp.float32
    brain_half_float = jnp.bfloat16
    highest_accuracy = lax.Precision.HIGHEST
    owners_count = lax.axis_size("adapter")
    seq_count = adapter_index_list.shape[2]
    capacity = max(2, seq_count // owners_count + 1)
    slot_total = owners_count * capacity
    hidden_state = forward_input[0]
    saved = stored_input[0]
    cotangent = output_gradient[0]
    weight = frozen_weight[0]
    down_factor_table = adapter_down_factor[0]
    up_factor_table = adapter_up_factor[0]
    adapters_held = down_factor_table.shape[0]
    rows, width = hidden_state.shape
    seq_len = rows // seq_count
    forward_base_output = jnp.dot(
        lax.all_gather(hidden_state, "mp", axis=1, tiled=True),
        weight,
        preferred_element_type=single_float,
    )
    mp_count = lax.axis_size("mp")
    z_count = mp_count // Y_RING
    block = weight.shape[0] // mp_count
    half_rows = cotangent.shape[0] * 13 // 32 // 8 * 8
    weight_y_major = (
        weight.reshape(z_count, Y_RING, block, weight.shape[1])
        .transpose(1, 0, 2, 3)
        .reshape(weight.shape)
    )
    contract = (((1,), (1,)), ((), ()))
    back_z_major = lax.dot_general(
        cotangent[:half_rows], weight, contract, preferred_element_type=single_float
    ).astype(jnp.bfloat16)
    back_y_major = lax.dot_general(
        cotangent[half_rows:], weight_y_major, contract, preferred_element_type=single_float
    ).astype(jnp.bfloat16)
    base_back = torus_reduce_scatter(back_z_major, back_y_major, "adapter", "mp")
    forward_placement, pick_fwd = pack_slots(
        adapter_index_list[0, 0], capacity, owners_count, adapters_held
    )
    placing_back, pick_back = pack_slots(
        adapter_index_list[1, 0], capacity, owners_count, adapters_held
    )

    def to_slots(placing, values):
        flat_rows = values.reshape(seq_count, seq_len * width)
        packed = jnp.dot(placing, flat_rows, preferred_element_type=single_float).astype(
            brain_half_float
        )
        return packed.reshape(owners_count, capacity, seq_len, width)

    def slots_gathered(placing, values):
        flat_rows = values.reshape(slot_total, seq_len * width)
        spread = lax.dot_general(
            placing, flat_rows, (((0,), (0,)), ((), ())), preferred_element_type=single_float
        )
        return spread.reshape(rows, width)

    send_fwd = to_slots(forward_placement, hidden_state)
    send_saved = to_slots(placing_back, saved)
    send_grad = to_slots(placing_back, cotangent)
    rows_fwd = lax.all_to_all(send_fwd, "adapter", split_axis=0, concat_axis=0, tiled=True)
    rows_saved = lax.all_to_all(send_saved, "adapter", split_axis=0, concat_axis=0, tiled=True)
    token_row_gradient = lax.all_to_all(
        send_grad, "adapter", split_axis=0, concat_axis=0, tiled=True
    )
    owner_fwd = lax.all_to_all(pick_fwd, "adapter", split_axis=0, concat_axis=0, tiled=True)
    owner_back = lax.all_to_all(pick_back, "adapter", split_axis=0, concat_axis=0, tiled=True)
    first_fwd = select_slabs(owner_fwd, down_factor_table)
    second_fwd = select_slabs(owner_fwd, up_factor_table)
    first_back = select_slabs(owner_back, down_factor_table)
    second_back = select_slabs(owner_back, up_factor_table)
    rank_fwd = jnp.einsum(
        "nklm,nkrm->nkrl", rows_fwd, first_fwd, preferred_element_type=single_float
    )
    rank_back = jnp.einsum(
        "nklm,nkrm->nkrl", rows_saved, first_back, preferred_element_type=single_float
    )
    rank_space_gradient = jnp.einsum(
        "nklm,nkrm->nkrl", token_row_gradient, second_back, preferred_element_type=single_float
    )
    rank_fwd, rank_back, rank_space_gradient = exchange_sum(
        (rank_fwd, rank_back, rank_space_gradient), "mp"
    )
    coded_fwd = rank_fwd.astype(brain_half_float)
    encoded_backward = rank_back.astype(brain_half_float)
    gradient_scaled = (adapter_scale * rank_space_gradient).astype(brain_half_float)
    adapter_token_rows = jnp.einsum(
        "nkrl,nkrm->nklm", coded_fwd, second_fwd, preferred_element_type=single_float
    ).astype(brain_half_float)
    back_rows = jnp.einsum(
        "nkrl,nkrm->nklm", gradient_scaled, first_back, preferred_element_type=single_float
    ).astype(brain_half_float)
    adapter_home_output = lax.all_to_all(
        adapter_token_rows, "adapter", split_axis=0, concat_axis=0, tiled=True
    )
    returned_home = lax.all_to_all(back_rows, "adapter", split_axis=0, concat_axis=0, tiled=True)
    slot_down_gradient = jnp.einsum(
        "nkrl,nklm->nkrm", gradient_scaled, rows_saved, preferred_element_type=single_float
    )
    slot_up_gradient = adapter_scale * jnp.einsum(
        "nkrl,nklm->nkrm", encoded_backward, token_row_gradient, preferred_element_type=single_float
    )
    adapter_home_output, returned_home, slot_down_gradient, slot_up_gradient, owner_selection = (
        adapter_home_output,
        returned_home,
        slot_down_gradient,
        slot_up_gradient,
        owner_back,
    )
    owner_weights = owner_selection.astype(single_float)
    grad_a = (
        jnp.einsum("nkj,nkrm->jrm", owner_weights, slot_down_gradient, precision=highest_accuracy)
        / seq_len
    ).astype(brain_half_float)
    grad_b = (
        jnp.einsum("nkj,nkrm->jrm", owner_weights, slot_up_gradient, precision=highest_accuracy)
        / seq_len
    ).astype(brain_half_float)
    adapter_sequence_output = slots_gathered(forward_placement, adapter_home_output)
    back_seq = slots_gathered(placing_back, returned_home)
    forward_output = (
        hidden_state.astype(single_float)
        + forward_base_output
        + adapter_scale * adapter_sequence_output
    ).astype(brain_half_float)
    out_back = (cotangent.astype(single_float) + base_back + back_seq).astype(brain_half_float)
    fwd_next = shifted(forward_output, "section", 1)
    back_next = shifted(out_back, "section", -1)
    return (fwd_next[None], back_next[None], grad_a[None], grad_b[None])


def solution(mesh):
    in_specs = (
        P("section", "adapter", "mp"),
        P("section", "adapter", "mp"),
        P("section", "adapter", "mp"),
        P("section", None, "mp"),
        P("section", "adapter", None, "mp"),
        P("section", "adapter", None, "mp"),
        P(None, "section", "adapter"),
    )
    out_specs = (
        P("section", "adapter", "mp"),
        P("section", "adapter", "mp"),
        P("section", "adapter", None, "mp"),
        P("section", "adapter", None, "mp"),
    )
    return jax.shard_map(local, mesh=mesh, in_specs=in_specs, out_specs=out_specs, check_vma=False)
```

```python
import jax
import jax.numpy as jnp
from jax import lax
from jax.sharding import PartitionSpec as P

adapter_scale = 2.0


def shifted(value, axis, steps):
    count = lax.axis_size(axis)
    pairs = [(source, (source + steps) % count) for source in range(count)]
    return lax.ppermute(value, axis, pairs)


def exchange(value, axis, bit):
    count = lax.axis_size(axis)
    pairs = [(source, source ^ (1 << bit)) for source in range(count)]
    return lax.ppermute(value, axis, pairs)


def halving_doubling_sum(values, axis):
    count = lax.axis_size(axis)
    levels = count.bit_length() - 1
    assert 1 << levels == count
    order = [0, 2, 1, 3, 4, 5, 6, 7, 8][:levels] if levels >= 3 else list(range(levels))
    order = [b for b in order if b < levels]
    me = lax.axis_index(axis)
    flat = jnp.concatenate([v.reshape(-1) for v in values])
    total = flat.shape[0]
    assert total % count == 0
    held = flat
    for bit in order:
        half = held.shape[0] // 2
        low, high = held[:half], held[half:]
        upper = ((me >> bit) & 1) == 1
        keep = jnp.where(upper, high, low)
        send = jnp.where(upper, low, high)
        held = keep + exchange(send, axis, bit)
    for bit in reversed(order):
        upper = ((me >> bit) & 1) == 1
        other = exchange(held, axis, bit)
        held = jnp.where(upper, jnp.concatenate([other, held]), jnp.concatenate([held, other]))
    pieces = []
    start = 0
    for v in values:
        pieces.append(held[start:start + v.size].reshape(v.shape))
        start += v.size
    return tuple(pieces)


Y_RING = 4


def ring_pairs(groups, count, z_step, y_step):
    z_count = count // Y_RING
    pairs = []
    for group in range(groups):
        sign = 1 if group % 2 == 0 else -1
        for source in range(count):
            z, y = divmod(source, Y_RING)
            target = ((z + sign * z_step) % z_count) * Y_RING + (y + sign * y_step) % Y_RING
            pairs.append((group * count + source, group * count + target))
    return pairs


def ring_reduce(partials, count, position, axes, pairs, sign, gate=None):
    width = partials.shape[1] // count

    def own(offset):
        index = (position - sign * offset + 2 * count) % count
        return lax.dynamic_slice_in_dim(partials, index * width, width, axis=1).astype(
            jnp.float32
        )

    total = own(1)
    for step in range(1, count):
        if gate is not None and step == count - 1:
            total, gate = lax.optimization_barrier((total, gate))
        arrived = lax.ppermute(total.astype(jnp.bfloat16), axes, pairs)
        total = arrived.astype(jnp.float32) + own(1 + step)
    return total


def torus_reduce_scatter(z_major, y_major, ring_axis, axis, gate=None):
    count = lax.axis_size(axis)
    z_count = count // Y_RING
    groups = lax.axis_size(ring_axis)
    axes = (ring_axis, axis)
    sign = 1 - 2 * (lax.axis_index(ring_axis) % 2)
    me = lax.axis_index(axis)
    z_me, y_me = me // Y_RING, me % Y_RING
    z_pairs = ring_pairs(groups, count, 1, 0)
    y_pairs = ring_pairs(groups, count, 0, 1)
    along_z = ring_reduce(z_major, z_count, z_me, axes, z_pairs, sign)
    first = ring_reduce(along_z, Y_RING, y_me, axes, y_pairs, sign, gate)
    along_y = ring_reduce(y_major, Y_RING, y_me, axes, y_pairs, sign)
    second = ring_reduce(along_y, z_count, z_me, axes, z_pairs, sign, gate)
    return jnp.concatenate([first, second], axis=0)


def exchange_sum(values, axis):
    count = lax.axis_size(axis)
    flat = jnp.concatenate([v.reshape(-1) for v in values])
    assert flat.shape[0] % count == 0
    pieces = lax.all_to_all(flat.reshape(count, -1), axis, 0, 0, tiled=True)
    reduced = jnp.sum(pieces, axis=0)
    spread = jnp.broadcast_to(reduced[None], pieces.shape)
    held = lax.all_to_all(spread, axis, 0, 0, tiled=True).reshape(-1)
    out = []
    start = 0
    for v in values:
        out.append(held[start:start + v.size].reshape(v.shape))
        start += v.size
    return tuple(out)


def pack_slots(ids_row, capacity, owners_count, adapters_held):
    seq_count = ids_row.shape[0]
    owners = ids_row // adapters_held
    positions = jnp.arange(seq_count, dtype=jnp.int32)
    same_owner = owners[:, None] == owners[None, :]
    earlier = positions[None, :] < positions[:, None]
    slot_rank = jnp.sum((same_owner & earlier).astype(jnp.int32), axis=1)
    slot_index = owners * capacity + slot_rank
    slot_ids = jnp.arange(owners_count * capacity, dtype=jnp.int32)
    placing = (slot_index[None, :] == slot_ids[:, None]).astype(jnp.bfloat16)
    local_ids = ids_row % adapters_held
    pick_seq = (local_ids[:, None] == jnp.arange(adapters_held, dtype=jnp.int32)[None, :]).astype(
        jnp.bfloat16
    )
    chosen = jnp.dot(placing, pick_seq, preferred_element_type=jnp.float32).astype(jnp.bfloat16)
    return (placing, chosen.reshape(owners_count, capacity, adapters_held))


def select_slabs(chosen, table):
    return jnp.einsum("nkj,jrm->nkrm", chosen, table, preferred_element_type=jnp.float32).astype(
        jnp.bfloat16
    )


def local(
    forward_input,
    stored_input,
    output_gradient,
    frozen_weight,
    adapter_down_factor,
    adapter_up_factor,
    adapter_index_list,
):
    single_float = jnp.float32
    brain_half_float = jnp.bfloat16
    highest_accuracy = lax.Precision.HIGHEST
    owners_count = lax.axis_size("adapter")
    seq_count = adapter_index_list.shape[2]
    capacity = max(2, seq_count // owners_count + 1)
    slot_total = owners_count * capacity
    hidden_state = forward_input[0]
    saved = stored_input[0]
    cotangent = output_gradient[0]
    weight = frozen_weight[0]
    down_factor_table = adapter_down_factor[0]
    up_factor_table = adapter_up_factor[0]
    adapters_held = down_factor_table.shape[0]
    rows, width = hidden_state.shape
    seq_len = rows // seq_count
    forward_base_output = jnp.dot(
        lax.all_gather(hidden_state, "mp", axis=1, tiled=True),
        weight,
        preferred_element_type=single_float,
    )
    mp_count = lax.axis_size("mp")
    z_count = mp_count // Y_RING
    block = weight.shape[0] // mp_count
    half_rows = cotangent.shape[0] * 13 // 32 // 8 * 8
    weight_y_major = (
        weight.reshape(z_count, Y_RING, block, weight.shape[1])
        .transpose(1, 0, 2, 3)
        .reshape(weight.shape)
    )
    contract = (((1,), (1,)), ((), ()))
    back_z_major = lax.dot_general(
        cotangent[:half_rows], weight, contract, preferred_element_type=single_float
    ).astype(jnp.bfloat16)
    back_y_major = lax.dot_general(
        cotangent[half_rows:], weight_y_major, contract, preferred_element_type=single_float
    ).astype(jnp.bfloat16)
    base_back = torus_reduce_scatter(
        back_z_major, back_y_major, "adapter", "mp", gate=forward_base_output
    )
    forward_placement, pick_fwd = pack_slots(
        adapter_index_list[0, 0], capacity, owners_count, adapters_held
    )
    placing_back, pick_back = pack_slots(
        adapter_index_list[1, 0], capacity, owners_count, adapters_held
    )

    def to_slots(placing, values):
        flat_rows = values.reshape(seq_count, seq_len * width)
        packed = jnp.dot(placing, flat_rows, preferred_element_type=single_float).astype(
            brain_half_float
        )
        return packed.reshape(owners_count, capacity, seq_len, width)

    def slots_gathered(placing, values):
        flat_rows = values.reshape(slot_total, seq_len * width)
        spread = lax.dot_general(
            placing, flat_rows, (((0,), (0,)), ((), ())), preferred_element_type=single_float
        )
        return spread.reshape(rows, width)

    send_fwd = to_slots(forward_placement, hidden_state)
    send_saved = to_slots(placing_back, saved)
    send_grad = to_slots(placing_back, cotangent)
    rows_fwd = lax.all_to_all(send_fwd, "adapter", split_axis=0, concat_axis=0, tiled=True)
    rows_saved = lax.all_to_all(send_saved, "adapter", split_axis=0, concat_axis=0, tiled=True)
    token_row_gradient = lax.all_to_all(
        send_grad, "adapter", split_axis=0, concat_axis=0, tiled=True
    )
    owner_fwd = lax.all_to_all(pick_fwd, "adapter", split_axis=0, concat_axis=0, tiled=True)
    owner_back = lax.all_to_all(pick_back, "adapter", split_axis=0, concat_axis=0, tiled=True)
    first_fwd = select_slabs(owner_fwd, down_factor_table)
    second_fwd = select_slabs(owner_fwd, up_factor_table)
    first_back = select_slabs(owner_back, down_factor_table)
    second_back = select_slabs(owner_back, up_factor_table)
    rank_fwd = jnp.einsum(
        "nklm,nkrm->nkrl", rows_fwd, first_fwd, preferred_element_type=single_float
    )
    rank_back = jnp.einsum(
        "nklm,nkrm->nkrl", rows_saved, first_back, preferred_element_type=single_float
    )
    rank_space_gradient = jnp.einsum(
        "nklm,nkrm->nkrl", token_row_gradient, second_back, preferred_element_type=single_float
    )
    rank_fwd, rank_back, rank_space_gradient = exchange_sum(
        (rank_fwd, rank_back, rank_space_gradient), "mp"
    )
    coded_fwd = rank_fwd.astype(brain_half_float)
    encoded_backward = rank_back.astype(brain_half_float)
    gradient_scaled = (adapter_scale * rank_space_gradient).astype(brain_half_float)
    adapter_token_rows = jnp.einsum(
        "nkrl,nkrm->nklm", coded_fwd, second_fwd, preferred_element_type=single_float
    ).astype(brain_half_float)
    back_rows = jnp.einsum(
        "nkrl,nkrm->nklm", gradient_scaled, first_back, preferred_element_type=single_float
    ).astype(brain_half_float)
    adapter_home_output = lax.all_to_all(
        adapter_token_rows, "adapter", split_axis=0, concat_axis=0, tiled=True
    )
    returned_home = lax.all_to_all(back_rows, "adapter", split_axis=0, concat_axis=0, tiled=True)
    slot_down_gradient = jnp.einsum(
        "nkrl,nklm->nkrm", gradient_scaled, rows_saved, preferred_element_type=single_float
    )
    slot_up_gradient = adapter_scale * jnp.einsum(
        "nkrl,nklm->nkrm", encoded_backward, token_row_gradient, preferred_element_type=single_float
    )
    adapter_home_output, returned_home, slot_down_gradient, slot_up_gradient, owner_selection = (
        adapter_home_output,
        returned_home,
        slot_down_gradient,
        slot_up_gradient,
        owner_back,
    )
    owner_weights = owner_selection.astype(single_float)
    grad_a = (
        jnp.einsum("nkj,nkrm->jrm", owner_weights, slot_down_gradient, precision=highest_accuracy)
        / seq_len
    ).astype(brain_half_float)
    grad_b = (
        jnp.einsum("nkj,nkrm->jrm", owner_weights, slot_up_gradient, precision=highest_accuracy)
        / seq_len
    ).astype(brain_half_float)
    adapter_sequence_output = slots_gathered(forward_placement, adapter_home_output)
    back_seq = slots_gathered(placing_back, returned_home)
    forward_output = (
        hidden_state.astype(single_float)
        + forward_base_output
        + adapter_scale * adapter_sequence_output
    ).astype(brain_half_float)
    out_back = (cotangent.astype(single_float) + base_back + back_seq).astype(brain_half_float)
    fwd_next = shifted(forward_output, "section", 1)
    back_next = shifted(out_back, "section", -1)
    return (fwd_next[None], back_next[None], grad_a[None], grad_b[None])


def solution(mesh):
    in_specs = (
        P("section", "adapter", "mp"),
        P("section", "adapter", "mp"),
        P("section", "adapter", "mp"),
        P("section", None, "mp"),
        P("section", "adapter", None, "mp"),
        P("section", "adapter", None, "mp"),
        P(None, "section", "adapter"),
    )
    out_specs = (
        P("section", "adapter", "mp"),
        P("section", "adapter", "mp"),
        P("section", "adapter", None, "mp"),
        P("section", "adapter", None, "mp"),
    )
    return jax.shard_map(local, mesh=mesh, in_specs=in_specs, out_specs=out_specs, check_vma=False)
```

```python
import jax
import jax.numpy as jnp
from jax import lax
from jax.sharding import PartitionSpec as P

adapter_scale = 2.0


def shifted(value, axis, steps):
    count = lax.axis_size(axis)
    pairs = [(source, (source + steps) % count) for source in range(count)]
    return lax.ppermute(value, axis, pairs)


def exchange(value, axis, bit):
    count = lax.axis_size(axis)
    pairs = [(source, source ^ (1 << bit)) for source in range(count)]
    return lax.ppermute(value, axis, pairs)


def halving_doubling_sum(values, axis):
    count = lax.axis_size(axis)
    levels = count.bit_length() - 1
    assert 1 << levels == count
    order = [0, 2, 1, 3, 4, 5, 6, 7, 8][:levels] if levels >= 3 else list(range(levels))
    order = [b for b in order if b < levels]
    me = lax.axis_index(axis)
    flat = jnp.concatenate([v.reshape(-1) for v in values])
    total = flat.shape[0]
    assert total % count == 0
    held = flat
    for bit in order:
        half = held.shape[0] // 2
        low, high = held[:half], held[half:]
        upper = ((me >> bit) & 1) == 1
        keep = jnp.where(upper, high, low)
        send = jnp.where(upper, low, high)
        held = keep + exchange(send, axis, bit)
    for bit in reversed(order):
        upper = ((me >> bit) & 1) == 1
        other = exchange(held, axis, bit)
        held = jnp.where(upper, jnp.concatenate([other, held]), jnp.concatenate([held, other]))
    pieces = []
    start = 0
    for v in values:
        pieces.append(held[start:start + v.size].reshape(v.shape))
        start += v.size
    return tuple(pieces)


Y_RING = 4


def ring_pairs(groups, count, z_step, y_step):
    z_count = count // Y_RING
    pairs = []
    for group in range(groups):
        sign = 1 if group % 2 == 0 else -1
        for source in range(count):
            z, y = divmod(source, Y_RING)
            target = ((z + sign * z_step) % z_count) * Y_RING + (y + sign * y_step) % Y_RING
            pairs.append((group * count + source, group * count + target))
    return pairs


def ring_reduce(partials, count, position, axes, pairs, sign, gate=None, gate_step=-1):
    width = partials.shape[1] // count

    def own(offset):
        index = (position - sign * offset + 2 * count) % count
        return lax.dynamic_slice_in_dim(partials, index * width, width, axis=1).astype(
            jnp.float32
        )

    total = own(1)
    for step in range(1, count):
        if gate is not None and step == gate_step % count:
            total, gate = lax.optimization_barrier((total, gate))
        arrived = lax.ppermute(total.astype(jnp.bfloat16), axes, pairs)
        total = arrived.astype(jnp.float32) + own(1 + step)
    return total


def torus_reduce_scatter(z_major, y_major, ring_axis, axis, gate=None):
    count = lax.axis_size(axis)
    z_count = count // Y_RING
    groups = lax.axis_size(ring_axis)
    axes = (ring_axis, axis)
    sign = 1 - 2 * (lax.axis_index(ring_axis) % 2)
    me = lax.axis_index(axis)
    z_me, y_me = me // Y_RING, me % Y_RING
    z_pairs = ring_pairs(groups, count, 1, 0)
    y_pairs = ring_pairs(groups, count, 0, 1)
    along_z = ring_reduce(z_major, z_count, z_me, axes, z_pairs, sign)
    first = ring_reduce(along_z, Y_RING, y_me, axes, y_pairs, sign, gate, 1)
    along_y = ring_reduce(y_major, Y_RING, y_me, axes, y_pairs, sign)
    second = ring_reduce(along_y, z_count, z_me, axes, z_pairs, sign, gate, -3)
    return jnp.concatenate([first, second], axis=0)


def exchange_sum(values, axis):
    count = lax.axis_size(axis)
    flat = jnp.concatenate([v.reshape(-1) for v in values])
    assert flat.shape[0] % count == 0
    pieces = lax.all_to_all(flat.reshape(count, -1), axis, 0, 0, tiled=True)
    reduced = jnp.sum(pieces, axis=0)
    spread = jnp.broadcast_to(reduced[None], pieces.shape)
    held = lax.all_to_all(spread, axis, 0, 0, tiled=True).reshape(-1)
    out = []
    start = 0
    for v in values:
        out.append(held[start:start + v.size].reshape(v.shape))
        start += v.size
    return tuple(out)


def pack_slots(ids_row, capacity, owners_count, adapters_held):
    seq_count = ids_row.shape[0]
    owners = ids_row // adapters_held
    positions = jnp.arange(seq_count, dtype=jnp.int32)
    same_owner = owners[:, None] == owners[None, :]
    earlier = positions[None, :] < positions[:, None]
    slot_rank = jnp.sum((same_owner & earlier).astype(jnp.int32), axis=1)
    slot_index = owners * capacity + slot_rank
    slot_ids = jnp.arange(owners_count * capacity, dtype=jnp.int32)
    placing = (slot_index[None, :] == slot_ids[:, None]).astype(jnp.bfloat16)
    local_ids = ids_row % adapters_held
    pick_seq = (local_ids[:, None] == jnp.arange(adapters_held, dtype=jnp.int32)[None, :]).astype(
        jnp.bfloat16
    )
    chosen = jnp.dot(placing, pick_seq, preferred_element_type=jnp.float32).astype(jnp.bfloat16)
    return (placing, chosen.reshape(owners_count, capacity, adapters_held))


def select_slabs(chosen, table):
    return jnp.einsum("nkj,jrm->nkrm", chosen, table, preferred_element_type=jnp.float32).astype(
        jnp.bfloat16
    )


def local(
    forward_input,
    stored_input,
    output_gradient,
    frozen_weight,
    adapter_down_factor,
    adapter_up_factor,
    adapter_index_list,
):
    single_float = jnp.float32
    brain_half_float = jnp.bfloat16
    highest_accuracy = lax.Precision.HIGHEST
    owners_count = lax.axis_size("adapter")
    seq_count = adapter_index_list.shape[2]
    capacity = max(2, seq_count // owners_count + 1)
    slot_total = owners_count * capacity
    hidden_state = forward_input[0]
    saved = stored_input[0]
    cotangent = output_gradient[0]
    weight = frozen_weight[0]
    down_factor_table = adapter_down_factor[0]
    up_factor_table = adapter_up_factor[0]
    adapters_held = down_factor_table.shape[0]
    rows, width = hidden_state.shape
    seq_len = rows // seq_count
    forward_base_output = jnp.dot(
        lax.all_gather(hidden_state, "mp", axis=1, tiled=True),
        weight,
        preferred_element_type=single_float,
    )
    mp_count = lax.axis_size("mp")
    z_count = mp_count // Y_RING
    block = weight.shape[0] // mp_count
    half_rows = cotangent.shape[0] * 13 // 32 // 8 * 8
    weight_y_major = (
        weight.reshape(z_count, Y_RING, block, weight.shape[1])
        .transpose(1, 0, 2, 3)
        .reshape(weight.shape)
    )
    contract = (((1,), (1,)), ((), ()))
    back_z_major = lax.dot_general(
        cotangent[:half_rows], weight, contract, preferred_element_type=single_float
    ).astype(jnp.bfloat16)
    back_y_major = lax.dot_general(
        cotangent[half_rows:], weight_y_major, contract, preferred_element_type=single_float
    ).astype(jnp.bfloat16)
    base_back = torus_reduce_scatter(
        back_z_major, back_y_major, "adapter", "mp", gate=forward_base_output
    )
    forward_placement, pick_fwd = pack_slots(
        adapter_index_list[0, 0], capacity, owners_count, adapters_held
    )
    placing_back, pick_back = pack_slots(
        adapter_index_list[1, 0], capacity, owners_count, adapters_held
    )

    def to_slots(placing, values):
        flat_rows = values.reshape(seq_count, seq_len * width)
        packed = jnp.dot(placing, flat_rows, preferred_element_type=single_float).astype(
            brain_half_float
        )
        return packed.reshape(owners_count, capacity, seq_len, width)

    def slots_gathered(placing, values):
        flat_rows = values.reshape(slot_total, seq_len * width)
        spread = lax.dot_general(
            placing, flat_rows, (((0,), (0,)), ((), ())), preferred_element_type=single_float
        )
        return spread.reshape(rows, width)

    send_fwd = to_slots(forward_placement, hidden_state)
    send_saved = to_slots(placing_back, saved)
    send_grad = to_slots(placing_back, cotangent)
    rows_fwd = lax.all_to_all(send_fwd, "adapter", split_axis=0, concat_axis=0, tiled=True)
    rows_saved = lax.all_to_all(send_saved, "adapter", split_axis=0, concat_axis=0, tiled=True)
    token_row_gradient = lax.all_to_all(
        send_grad, "adapter", split_axis=0, concat_axis=0, tiled=True
    )
    owner_fwd = lax.all_to_all(pick_fwd, "adapter", split_axis=0, concat_axis=0, tiled=True)
    owner_back = lax.all_to_all(pick_back, "adapter", split_axis=0, concat_axis=0, tiled=True)
    first_fwd = select_slabs(owner_fwd, down_factor_table)
    second_fwd = select_slabs(owner_fwd, up_factor_table)
    first_back = select_slabs(owner_back, down_factor_table)
    second_back = select_slabs(owner_back, up_factor_table)
    rank_fwd = jnp.einsum(
        "nklm,nkrm->nkrl", rows_fwd, first_fwd, preferred_element_type=single_float
    )
    rank_back = jnp.einsum(
        "nklm,nkrm->nkrl", rows_saved, first_back, preferred_element_type=single_float
    )
    rank_space_gradient = jnp.einsum(
        "nklm,nkrm->nkrl", token_row_gradient, second_back, preferred_element_type=single_float
    )
    rank_fwd, rank_back, rank_space_gradient = exchange_sum(
        (rank_fwd, rank_back, rank_space_gradient), "mp"
    )
    coded_fwd = rank_fwd.astype(brain_half_float)
    encoded_backward = rank_back.astype(brain_half_float)
    gradient_scaled = (adapter_scale * rank_space_gradient).astype(brain_half_float)
    adapter_token_rows = jnp.einsum(
        "nkrl,nkrm->nklm", coded_fwd, second_fwd, preferred_element_type=single_float
    ).astype(brain_half_float)
    back_rows = jnp.einsum(
        "nkrl,nkrm->nklm", gradient_scaled, first_back, preferred_element_type=single_float
    ).astype(brain_half_float)
    adapter_home_output = lax.all_to_all(
        adapter_token_rows, "adapter", split_axis=0, concat_axis=0, tiled=True
    )
    returned_home = lax.all_to_all(back_rows, "adapter", split_axis=0, concat_axis=0, tiled=True)
    slot_down_gradient = jnp.einsum(
        "nkrl,nklm->nkrm", gradient_scaled, rows_saved, preferred_element_type=single_float
    )
    slot_up_gradient = adapter_scale * jnp.einsum(
        "nkrl,nklm->nkrm", encoded_backward, token_row_gradient, preferred_element_type=single_float
    )
    adapter_home_output, returned_home, slot_down_gradient, slot_up_gradient, owner_selection = (
        adapter_home_output,
        returned_home,
        slot_down_gradient,
        slot_up_gradient,
        owner_back,
    )
    owner_weights = owner_selection.astype(single_float)
    grad_a = (
        jnp.einsum("nkj,nkrm->jrm", owner_weights, slot_down_gradient, precision=highest_accuracy)
        / seq_len
    ).astype(brain_half_float)
    grad_b = (
        jnp.einsum("nkj,nkrm->jrm", owner_weights, slot_up_gradient, precision=highest_accuracy)
        / seq_len
    ).astype(brain_half_float)
    adapter_sequence_output = slots_gathered(forward_placement, adapter_home_output)
    back_seq = slots_gathered(placing_back, returned_home)
    forward_output = (
        hidden_state.astype(single_float)
        + forward_base_output
        + adapter_scale * adapter_sequence_output
    ).astype(brain_half_float)
    out_back = (cotangent.astype(single_float) + base_back + back_seq).astype(brain_half_float)
    fwd_next = shifted(forward_output, "section", 1)
    back_next = shifted(out_back, "section", -1)
    return (fwd_next[None], back_next[None], grad_a[None], grad_b[None])


def solution(mesh):
    in_specs = (
        P("section", "adapter", "mp"),
        P("section", "adapter", "mp"),
        P("section", "adapter", "mp"),
        P("section", None, "mp"),
        P("section", "adapter", None, "mp"),
        P("section", "adapter", None, "mp"),
        P(None, "section", "adapter"),
    )
    out_specs = (
        P("section", "adapter", "mp"),
        P("section", "adapter", "mp"),
        P("section", "adapter", None, "mp"),
        P("section", "adapter", None, "mp"),
    )
    return jax.shard_map(local, mesh=mesh, in_specs=in_specs, out_specs=out_specs, check_vma=False)
```

```python
import jax
import jax.numpy as jnp
from jax import lax
from jax.sharding import PartitionSpec as P

adapter_scale = 2.0


def shifted(value, axis, steps):
    count = lax.axis_size(axis)
    pairs = [(source, (source + steps) % count) for source in range(count)]
    return lax.ppermute(value, axis, pairs)


def exchange(value, axis, bit):
    count = lax.axis_size(axis)
    pairs = [(source, source ^ (1 << bit)) for source in range(count)]
    return lax.ppermute(value, axis, pairs)


def halving_doubling_sum(values, axis):
    count = lax.axis_size(axis)
    levels = count.bit_length() - 1
    assert 1 << levels == count
    order = [0, 2, 1, 3, 4, 5, 6, 7, 8][:levels] if levels >= 3 else list(range(levels))
    order = [b for b in order if b < levels]
    me = lax.axis_index(axis)
    flat = jnp.concatenate([v.reshape(-1) for v in values])
    total = flat.shape[0]
    assert total % count == 0
    held = flat
    for bit in order:
        half = held.shape[0] // 2
        low, high = held[:half], held[half:]
        upper = ((me >> bit) & 1) == 1
        keep = jnp.where(upper, high, low)
        send = jnp.where(upper, low, high)
        held = keep + exchange(send, axis, bit)
    for bit in reversed(order):
        upper = ((me >> bit) & 1) == 1
        other = exchange(held, axis, bit)
        held = jnp.where(upper, jnp.concatenate([other, held]), jnp.concatenate([held, other]))
    pieces = []
    start = 0
    for v in values:
        pieces.append(held[start:start + v.size].reshape(v.shape))
        start += v.size
    return tuple(pieces)


Y_RING = 4


def ring_pairs(groups, count, z_step, y_step):
    z_count = count // Y_RING
    pairs = []
    for group in range(groups):
        sign = 1 if group % 2 == 0 else -1
        for source in range(count):
            z, y = divmod(source, Y_RING)
            target = ((z + sign * z_step) % z_count) * Y_RING + (y + sign * y_step) % Y_RING
            pairs.append((group * count + source, group * count + target))
    return pairs


def ring_reduce(partials, count, position, axes, pairs, sign):
    width = partials.shape[1] // count

    def own(offset):
        index = (position - sign * offset + 2 * count) % count
        return lax.dynamic_slice_in_dim(partials, index * width, width, axis=1).astype(
            jnp.float32
        )

    total = own(1)
    for step in range(1, count):
        arrived = lax.ppermute(total.astype(jnp.bfloat16), axes, pairs)
        total = arrived.astype(jnp.float32) + own(1 + step)
    return total


def torus_reduce_scatter(z_major, y_major, ring_axis, axis):
    count = lax.axis_size(axis)
    z_count = count // Y_RING
    groups = lax.axis_size(ring_axis)
    axes = (ring_axis, axis)
    sign = 1 - 2 * (lax.axis_index(ring_axis) % 2)
    me = lax.axis_index(axis)
    z_me, y_me = me // Y_RING, me % Y_RING
    z_pairs = ring_pairs(groups, count, 1, 0)
    y_pairs = ring_pairs(groups, count, 0, 1)
    along_z = ring_reduce(z_major, z_count, z_me, axes, z_pairs, sign)
    first = ring_reduce(along_z, Y_RING, y_me, axes, y_pairs, sign)
    along_y = ring_reduce(y_major, Y_RING, y_me, axes, y_pairs, sign)
    second = ring_reduce(along_y, z_count, z_me, axes, z_pairs, sign)
    return jnp.concatenate([first, second], axis=0)


def exchange_sum(values, axis):
    count = lax.axis_size(axis)
    flat = jnp.concatenate([v.reshape(-1) for v in values])
    assert flat.shape[0] % count == 0
    pieces = lax.all_to_all(flat.reshape(count, -1), axis, 0, 0, tiled=True)
    reduced = jnp.sum(pieces, axis=0)
    spread = jnp.broadcast_to(reduced[None], pieces.shape)
    held = lax.all_to_all(spread, axis, 0, 0, tiled=True).reshape(-1)
    out = []
    start = 0
    for v in values:
        out.append(held[start:start + v.size].reshape(v.shape))
        start += v.size
    return tuple(out)


def pack_slots(ids_row, capacity, owners_count, adapters_held):
    seq_count = ids_row.shape[0]
    owners = ids_row // adapters_held
    positions = jnp.arange(seq_count, dtype=jnp.int32)
    same_owner = owners[:, None] == owners[None, :]
    earlier = positions[None, :] < positions[:, None]
    slot_rank = jnp.sum((same_owner & earlier).astype(jnp.int32), axis=1)
    slot_index = owners * capacity + slot_rank
    slot_ids = jnp.arange(owners_count * capacity, dtype=jnp.int32)
    placing = (slot_index[None, :] == slot_ids[:, None]).astype(jnp.bfloat16)
    local_ids = ids_row % adapters_held
    pick_seq = (local_ids[:, None] == jnp.arange(adapters_held, dtype=jnp.int32)[None, :]).astype(
        jnp.bfloat16
    )
    chosen = jnp.dot(placing, pick_seq, preferred_element_type=jnp.float32).astype(jnp.bfloat16)
    return (placing, chosen.reshape(owners_count, capacity, adapters_held))


def select_slabs(chosen, table):
    return jnp.einsum("nkj,jrm->nkrm", chosen, table, preferred_element_type=jnp.float32).astype(
        jnp.bfloat16
    )


def local(
    forward_input,
    stored_input,
    output_gradient,
    frozen_weight,
    adapter_down_factor,
    adapter_up_factor,
    adapter_index_list,
):
    single_float = jnp.float32
    brain_half_float = jnp.bfloat16
    highest_accuracy = lax.Precision.HIGHEST
    owners_count = lax.axis_size("adapter")
    seq_count = adapter_index_list.shape[2]
    capacity = max(2, seq_count // owners_count + 1)
    slot_total = owners_count * capacity
    hidden_state = forward_input[0]
    saved = stored_input[0]
    cotangent = output_gradient[0]
    weight = frozen_weight[0]
    down_factor_table = adapter_down_factor[0]
    up_factor_table = adapter_up_factor[0]
    adapters_held = down_factor_table.shape[0]
    rows, width = hidden_state.shape
    seq_len = rows // seq_count
    forward_base_output = jnp.dot(
        lax.all_gather(hidden_state, "mp", axis=1, tiled=True),
        weight,
        preferred_element_type=single_float,
    )
    mp_count = lax.axis_size("mp")
    z_count = mp_count // Y_RING
    block = weight.shape[0] // mp_count
    half_rows = cotangent.shape[0] * 13 // 32 // 8 * 8
    weight_y_major = (
        weight.reshape(z_count, Y_RING, block, weight.shape[1])
        .transpose(1, 0, 2, 3)
        .reshape(weight.shape)
    )
    contract = (((1,), (1,)), ((), ()))
    back_z_major = lax.dot_general(
        cotangent[:half_rows], weight, contract, preferred_element_type=single_float
    ).astype(jnp.bfloat16)
    back_y_major = lax.dot_general(
        cotangent[half_rows:], weight_y_major, contract, preferred_element_type=single_float
    ).astype(jnp.bfloat16)
    base_back = torus_reduce_scatter(back_z_major, back_y_major, "adapter", "mp")
    forward_placement, pick_fwd = pack_slots(
        adapter_index_list[0, 0], capacity, owners_count, adapters_held
    )
    placing_back, pick_back = pack_slots(
        adapter_index_list[1, 0], capacity, owners_count, adapters_held
    )

    def to_slots(placing, values):
        flat_rows = values.reshape(seq_count, seq_len * width)
        packed = jnp.dot(placing, flat_rows, preferred_element_type=single_float).astype(
            brain_half_float
        )
        return packed.reshape(owners_count, capacity, seq_len, width)

    def slots_gathered(placing, values):
        slot_rows = values.reshape(slot_total, seq_len, width)
        spread = jnp.einsum("sq,slw->qlw", placing, slot_rows, preferred_element_type=single_float)
        return spread.reshape(rows, width)

    send_fwd = to_slots(forward_placement, hidden_state)
    send_saved = to_slots(placing_back, saved)
    send_grad = to_slots(placing_back, cotangent)
    rows_fwd = lax.all_to_all(send_fwd, "adapter", split_axis=0, concat_axis=0, tiled=True)
    rows_saved = lax.all_to_all(send_saved, "adapter", split_axis=0, concat_axis=0, tiled=True)
    token_row_gradient = lax.all_to_all(
        send_grad, "adapter", split_axis=0, concat_axis=0, tiled=True
    )
    owner_fwd = lax.all_to_all(pick_fwd, "adapter", split_axis=0, concat_axis=0, tiled=True)
    owner_back = lax.all_to_all(pick_back, "adapter", split_axis=0, concat_axis=0, tiled=True)
    first_fwd = select_slabs(owner_fwd, down_factor_table)
    second_fwd = select_slabs(owner_fwd, up_factor_table)
    first_back = select_slabs(owner_back, down_factor_table)
    second_back = select_slabs(owner_back, up_factor_table)
    rank_fwd = jnp.einsum(
        "nklm,nkrm->nkrl", rows_fwd, first_fwd, preferred_element_type=single_float
    )
    rank_back = jnp.einsum(
        "nklm,nkrm->nkrl", rows_saved, first_back, preferred_element_type=single_float
    )
    rank_space_gradient = jnp.einsum(
        "nklm,nkrm->nkrl", token_row_gradient, second_back, preferred_element_type=single_float
    )
    rank_fwd, rank_back, rank_space_gradient = exchange_sum(
        (rank_fwd, rank_back, rank_space_gradient), "mp"
    )
    coded_fwd = rank_fwd.astype(brain_half_float)
    encoded_backward = rank_back.astype(brain_half_float)
    gradient_scaled = (adapter_scale * rank_space_gradient).astype(brain_half_float)
    adapter_token_rows = jnp.einsum(
        "nkrl,nkrm->nklm", coded_fwd, second_fwd, preferred_element_type=single_float
    ).astype(brain_half_float)
    back_rows = jnp.einsum(
        "nkrl,nkrm->nklm", gradient_scaled, first_back, preferred_element_type=single_float
    ).astype(brain_half_float)
    adapter_home_output = lax.all_to_all(
        adapter_token_rows, "adapter", split_axis=0, concat_axis=0, tiled=True
    )
    returned_home = lax.all_to_all(back_rows, "adapter", split_axis=0, concat_axis=0, tiled=True)
    slot_down_gradient = jnp.einsum(
        "nkrl,nklm->nkrm", gradient_scaled, rows_saved, preferred_element_type=single_float
    )
    slot_up_gradient = adapter_scale * jnp.einsum(
        "nkrl,nklm->nkrm", encoded_backward, token_row_gradient, preferred_element_type=single_float
    )
    adapter_home_output, returned_home, slot_down_gradient, slot_up_gradient, owner_selection = (
        adapter_home_output,
        returned_home,
        slot_down_gradient,
        slot_up_gradient,
        owner_back,
    )
    owner_weights = owner_selection.astype(single_float)
    grad_a = (
        jnp.einsum("nkj,nkrm->jrm", owner_weights, slot_down_gradient, precision=highest_accuracy)
        / seq_len
    ).astype(brain_half_float)
    grad_b = (
        jnp.einsum("nkj,nkrm->jrm", owner_weights, slot_up_gradient, precision=highest_accuracy)
        / seq_len
    ).astype(brain_half_float)
    adapter_sequence_output = slots_gathered(forward_placement, adapter_home_output)
    back_seq = slots_gathered(placing_back, returned_home)
    forward_output = (
        hidden_state.astype(single_float)
        + forward_base_output
        + adapter_scale * adapter_sequence_output
    ).astype(brain_half_float)
    out_back = (cotangent.astype(single_float) + base_back + back_seq).astype(brain_half_float)
    fwd_next = shifted(forward_output, "section", 1)
    back_next = shifted(out_back, "section", -1)
    return (fwd_next[None], back_next[None], grad_a[None], grad_b[None])


def solution(mesh):
    in_specs = (
        P("section", "adapter", "mp"),
        P("section", "adapter", "mp"),
        P("section", "adapter", "mp"),
        P("section", None, "mp"),
        P("section", "adapter", None, "mp"),
        P("section", "adapter", None, "mp"),
        P(None, "section", "adapter"),
    )
    out_specs = (
        P("section", "adapter", "mp"),
        P("section", "adapter", "mp"),
        P("section", "adapter", None, "mp"),
        P("section", "adapter", None, "mp"),
    )
    return jax.shard_map(local, mesh=mesh, in_specs=in_specs, out_specs=out_specs, check_vma=False)
```

```python
import jax
import jax.numpy as jnp
from jax import lax
from jax.sharding import PartitionSpec as P

adapter_scale = 2.0


def shifted(value, axis, steps):
    count = lax.axis_size(axis)
    pairs = [(source, (source + steps) % count) for source in range(count)]
    return lax.ppermute(value, axis, pairs)


def exchange(value, axis, bit):
    count = lax.axis_size(axis)
    pairs = [(source, source ^ (1 << bit)) for source in range(count)]
    return lax.ppermute(value, axis, pairs)


def halving_doubling_sum(values, axis):
    count = lax.axis_size(axis)
    levels = count.bit_length() - 1
    assert 1 << levels == count
    order = [0, 2, 1, 3, 4, 5, 6, 7, 8][:levels] if levels >= 3 else list(range(levels))
    order = [b for b in order if b < levels]
    me = lax.axis_index(axis)
    flat = jnp.concatenate([v.reshape(-1) for v in values])
    total = flat.shape[0]
    assert total % count == 0
    held = flat
    for bit in order:
        half = held.shape[0] // 2
        low, high = held[:half], held[half:]
        upper = ((me >> bit) & 1) == 1
        keep = jnp.where(upper, high, low)
        send = jnp.where(upper, low, high)
        held = keep + exchange(send, axis, bit)
    for bit in reversed(order):
        upper = ((me >> bit) & 1) == 1
        other = exchange(held, axis, bit)
        held = jnp.where(upper, jnp.concatenate([other, held]), jnp.concatenate([held, other]))
    pieces = []
    start = 0
    for v in values:
        pieces.append(held[start:start + v.size].reshape(v.shape))
        start += v.size
    return tuple(pieces)


Y_RING = 4


def ring_pairs(groups, count, z_step, y_step):
    z_count = count // Y_RING
    pairs = []
    for group in range(groups):
        sign = 1 if group % 2 == 0 else -1
        for source in range(count):
            z, y = divmod(source, Y_RING)
            target = ((z + sign * z_step) % z_count) * Y_RING + (y + sign * y_step) % Y_RING
            pairs.append((group * count + source, group * count + target))
    return pairs


def ring_reduce(partials, count, position, axes, pairs, sign):
    width = partials.shape[1] // count

    def own(offset):
        index = (position - sign * offset + 2 * count) % count
        return lax.dynamic_slice_in_dim(partials, index * width, width, axis=1).astype(
            jnp.float32
        )

    total = own(1)
    for step in range(1, count):
        arrived = lax.ppermute(total.astype(jnp.bfloat16), axes, pairs)
        total = arrived.astype(jnp.float32) + own(1 + step)
    return total


def torus_reduce_scatter(z_major, y_major, ring_axis, axis):
    count = lax.axis_size(axis)
    z_count = count // Y_RING
    groups = lax.axis_size(ring_axis)
    axes = (ring_axis, axis)
    sign = 1 - 2 * (lax.axis_index(ring_axis) % 2)
    me = lax.axis_index(axis)
    z_me, y_me = me // Y_RING, me % Y_RING
    z_pairs = ring_pairs(groups, count, 1, 0)
    y_pairs = ring_pairs(groups, count, 0, 1)
    along_z = ring_reduce(z_major, z_count, z_me, axes, z_pairs, sign)
    first = ring_reduce(along_z, Y_RING, y_me, axes, y_pairs, sign)
    along_y = ring_reduce(y_major, Y_RING, y_me, axes, y_pairs, sign)
    second = ring_reduce(along_y, z_count, z_me, axes, z_pairs, sign)
    return jnp.concatenate([first, second], axis=0)


def exchange_sum(values, axis):
    count = lax.axis_size(axis)
    flat = jnp.concatenate([v.reshape(-1) for v in values])
    assert flat.shape[0] % count == 0
    pieces = lax.all_to_all(flat.reshape(count, -1), axis, 0, 0, tiled=True)
    reduced = jnp.sum(pieces, axis=0)
    spread = jnp.broadcast_to(reduced[None], pieces.shape)
    held = lax.all_to_all(spread, axis, 0, 0, tiled=True).reshape(-1)
    out = []
    start = 0
    for v in values:
        out.append(held[start:start + v.size].reshape(v.shape))
        start += v.size
    return tuple(out)


def pack_slots(ids_row, capacity, owners_count, adapters_held):
    seq_count = ids_row.shape[0]
    owners = ids_row // adapters_held
    positions = jnp.arange(seq_count, dtype=jnp.int32)
    same_owner = owners[:, None] == owners[None, :]
    earlier = positions[None, :] < positions[:, None]
    slot_rank = jnp.sum((same_owner & earlier).astype(jnp.int32), axis=1)
    slot_index = owners * capacity + slot_rank
    slot_ids = jnp.arange(owners_count * capacity, dtype=jnp.int32)
    placing = (slot_index[None, :] == slot_ids[:, None]).astype(jnp.bfloat16)
    local_ids = ids_row % adapters_held
    pick_seq = (local_ids[:, None] == jnp.arange(adapters_held, dtype=jnp.int32)[None, :]).astype(
        jnp.bfloat16
    )
    chosen = jnp.dot(placing, pick_seq, preferred_element_type=jnp.float32).astype(jnp.bfloat16)
    return (placing, chosen.reshape(owners_count, capacity, adapters_held))


def select_slabs(chosen, table):
    return jnp.einsum("nkj,jrm->nkrm", chosen, table, preferred_element_type=jnp.float32).astype(
        jnp.bfloat16
    )


def local(
    forward_input,
    stored_input,
    output_gradient,
    frozen_weight,
    adapter_down_factor,
    adapter_up_factor,
    adapter_index_list,
):
    single_float = jnp.float32
    brain_half_float = jnp.bfloat16
    highest_accuracy = lax.Precision.HIGHEST
    owners_count = lax.axis_size("adapter")
    seq_count = adapter_index_list.shape[2]
    capacity = max(2, seq_count // owners_count + 1)
    slot_total = owners_count * capacity
    hidden_state = forward_input[0]
    saved = stored_input[0]
    cotangent = output_gradient[0]
    weight = frozen_weight[0]
    down_factor_table = adapter_down_factor[0]
    up_factor_table = adapter_up_factor[0]
    adapters_held = down_factor_table.shape[0]
    rows, width = hidden_state.shape
    seq_len = rows // seq_count
    forward_base_output = jnp.dot(
        lax.all_gather(hidden_state, "mp", axis=1, tiled=True),
        weight,
        preferred_element_type=single_float,
    )
    mp_count = lax.axis_size("mp")
    z_count = mp_count // Y_RING
    block = weight.shape[0] // mp_count
    half_rows = cotangent.shape[0] * 13 // 32 // 8 * 8
    weight_y_major = (
        weight.reshape(z_count, Y_RING, block, weight.shape[1])
        .transpose(1, 0, 2, 3)
        .reshape(weight.shape)
    )
    contract = (((1,), (1,)), ((), ()))
    back_z_major = lax.dot_general(
        cotangent[:half_rows], weight, contract, preferred_element_type=single_float
    ).astype(jnp.bfloat16)
    back_y_major = lax.dot_general(
        cotangent[half_rows:], weight_y_major, contract, preferred_element_type=single_float
    ).astype(jnp.bfloat16)
    base_back = torus_reduce_scatter(back_z_major, back_y_major, "adapter", "mp")
    forward_placement, pick_fwd = pack_slots(
        adapter_index_list[0, 0], capacity, owners_count, adapters_held
    )
    placing_back, pick_back = pack_slots(
        adapter_index_list[1, 0], capacity, owners_count, adapters_held
    )

    def to_slots(placing, values):
        flat_rows = values.reshape(seq_count, seq_len * width)
        packed = jnp.dot(placing, flat_rows, preferred_element_type=single_float).astype(
            brain_half_float
        )
        return packed.reshape(owners_count, capacity, seq_len, width)

    def slots_gathered(placing, values):
        flat_rows = values.reshape(slot_total, seq_len * width)
        spread = lax.dot_general(
            placing, flat_rows, (((0,), (0,)), ((), ())), preferred_element_type=single_float
        )
        return spread.reshape(rows, width)

    send_fwd = to_slots(forward_placement, hidden_state)
    send_saved = to_slots(placing_back, saved)
    send_grad = to_slots(placing_back, cotangent)
    rows_fwd = lax.all_to_all(send_fwd, "adapter", split_axis=0, concat_axis=0, tiled=True)
    rows_saved = lax.all_to_all(send_saved, "adapter", split_axis=0, concat_axis=0, tiled=True)
    token_row_gradient = lax.all_to_all(
        send_grad, "adapter", split_axis=0, concat_axis=0, tiled=True
    )
    owner_fwd = lax.all_to_all(pick_fwd, "adapter", split_axis=0, concat_axis=0, tiled=True)
    owner_back = lax.all_to_all(pick_back, "adapter", split_axis=0, concat_axis=0, tiled=True)
    first_fwd = select_slabs(owner_fwd, down_factor_table)
    second_fwd = select_slabs(owner_fwd, up_factor_table)
    first_back = select_slabs(owner_back, down_factor_table)
    second_back = select_slabs(owner_back, up_factor_table)
    rank_fwd = jnp.einsum(
        "nklm,nkrm->nkrl", rows_fwd, first_fwd, preferred_element_type=single_float
    )
    rank_back = jnp.einsum(
        "nklm,nkrm->nkrl", rows_saved, first_back, preferred_element_type=single_float
    )
    rank_space_gradient = jnp.einsum(
        "nklm,nkrm->nkrl", token_row_gradient, second_back, preferred_element_type=single_float
    )
    rank_fwd, rank_back, rank_space_gradient = exchange_sum(
        (rank_fwd, rank_back, rank_space_gradient), "mp"
    )
    coded_fwd = rank_fwd.astype(brain_half_float)
    encoded_backward = rank_back.astype(brain_half_float)
    gradient_scaled = (adapter_scale * rank_space_gradient).astype(brain_half_float)
    adapter_token_rows = jnp.einsum(
        "nkrl,nkrm->nklm", coded_fwd, second_fwd, preferred_element_type=single_float
    ).astype(brain_half_float)
    back_rows = jnp.einsum(
        "nkrl,nkrm->nklm", gradient_scaled, first_back, preferred_element_type=single_float
    ).astype(brain_half_float)
    both_home = lax.all_to_all(
        jnp.stack([adapter_token_rows, back_rows], axis=1),
        "adapter",
        split_axis=0,
        concat_axis=0,
        tiled=True,
    )
    adapter_home_output = both_home[:, 0]
    returned_home = both_home[:, 1]
    slot_down_gradient = jnp.einsum(
        "nkrl,nklm->nkrm", gradient_scaled, rows_saved, preferred_element_type=single_float
    )
    slot_up_gradient = adapter_scale * jnp.einsum(
        "nkrl,nklm->nkrm", encoded_backward, token_row_gradient, preferred_element_type=single_float
    )
    adapter_home_output, returned_home, slot_down_gradient, slot_up_gradient, owner_selection = (
        adapter_home_output,
        returned_home,
        slot_down_gradient,
        slot_up_gradient,
        owner_back,
    )
    owner_weights = owner_selection.astype(single_float)
    grad_a = (
        jnp.einsum("nkj,nkrm->jrm", owner_weights, slot_down_gradient, precision=highest_accuracy)
        / seq_len
    ).astype(brain_half_float)
    grad_b = (
        jnp.einsum("nkj,nkrm->jrm", owner_weights, slot_up_gradient, precision=highest_accuracy)
        / seq_len
    ).astype(brain_half_float)
    adapter_sequence_output = slots_gathered(forward_placement, adapter_home_output)
    back_seq = slots_gathered(placing_back, returned_home)
    forward_output = (
        hidden_state.astype(single_float)
        + forward_base_output
        + adapter_scale * adapter_sequence_output
    ).astype(brain_half_float)
    out_back = (cotangent.astype(single_float) + base_back + back_seq).astype(brain_half_float)
    fwd_next = shifted(forward_output, "section", 1)
    back_next = shifted(out_back, "section", -1)
    return (fwd_next[None], back_next[None], grad_a[None], grad_b[None])


def solution(mesh):
    in_specs = (
        P("section", "adapter", "mp"),
        P("section", "adapter", "mp"),
        P("section", "adapter", "mp"),
        P("section", None, "mp"),
        P("section", "adapter", None, "mp"),
        P("section", "adapter", None, "mp"),
        P(None, "section", "adapter"),
    )
    out_specs = (
        P("section", "adapter", "mp"),
        P("section", "adapter", "mp"),
        P("section", "adapter", None, "mp"),
        P("section", "adapter", None, "mp"),
    )
    return jax.shard_map(local, mesh=mesh, in_specs=in_specs, out_specs=out_specs, check_vma=False)
```
